256 devices in a mesh: rows: 32 (over x, z_lo, y), cols: 8 (over z_hi, core).
Axes of the slice: x: 4, y: 4, z: 8 (z_hi: 4, z_lo: 2; z = z_hi * 2 + z_lo), core: 2. Of those that a mesh axis runs over, the one named last changes fastest.
Arguments:
- state: float32 [9, 1024, 4096], P(None, 'rows', 'cols'), may hold values from -3.5 to 7.2, as said below
- hardness: int32 [1024, 4096], P('rows', 'cols'), may hold values from 0 to 3
- rain_mask: int32 [1024, 4096], P('rows', 'cols'), may hold values from 0 to 1
Outputs:
- final_state: float32 [9, 1024, 4096], P(None, 'rows', 'cols')
The draws below stay inside these ranges and needn't reach their ends.
Inputs may be any that keep to these rules, and one draw needn't show every extreme that they name: `state`: water depth, sediment and outflows are nonnegative.
All inputs are finite; a program needn't handle non-finite values.
Results may differ from the reference program's by a relative error of at most 0.0003.
Values sent between devices are 32-bit elements; how exact they have to be, the bound alone decides.
No kernel may reach another device: no remote copies, remote signals or barrier semaphores. Data moves between devices by JAX's collectives and lax.ppermute only.
A program may use at most 64 MiB of HBM per device.

```python
import jax
import jax.numpy as jnp
from jax import lax

STEPS = 8
NX = 1024
NY = 4096


def draw_state(key, part):
    keys = jax.random.split(key, 5)
    rows = (jnp.arange(NX, dtype=jnp.float32) / NX)[:, None]
    rise = 1.0 + 2.0 * rows
    height = jnp.clip(jax.random.normal(keys[0], (NX, NY), jnp.float32), -3.5, 3.5)
    water = jax.random.uniform(keys[1], (NX, NY), jnp.float32, 0.2, 1.0) * rise
    sediment = jax.random.uniform(keys[2], (NX, NY), jnp.float32, 0.0, 0.3)
    outflows = jax.random.uniform(keys[3], (4, NX, NY), jnp.float32, 0.0, 0.4)
    motion = jnp.clip(0.5 * jax.random.normal(keys[4], (2, NX, NY), jnp.float32), -2.0, 2.0)
    return jnp.concatenate([height[None], water[None], sediment[None], outflows, motion], axis=0)


def draw_rain_mask(key, part):
    picks = jax.random.randint(key, (NX, NY), 0, 1024)
    rows = jnp.arange(NX, dtype=jnp.int32)[:, None]
    limit = 128 + 256 * rows // NX
    return (picks < limit).astype(jnp.int32)


def with_ends(drawn, stream_key, smallest, largest):
    index_at = [jax.random.randint(jax.random.fold_in(stream_key, axis), (), 0, length) for axis, length in enumerate(drawn.shape)]
    widest = drawn.shape.index(max(drawn.shape))
    neighbour = index_at[:widest] + [(index_at[widest] + 1) % drawn.shape[widest]] + index_at[widest + 1:]
    return drawn.at[tuple(index_at)].set(smallest).at[tuple(neighbour)].set(largest)


def setup_inputs(seed: int = 0) -> dict:
    key_of = jax.random.split(jax.random.key(seed), 4)
    return {
        "state": draw_state(jax.random.fold_in(key_of[3], 71), 0),
        "hardness": with_ends(jax.random.randint(key_of[1], (NX, NY), 0, 4), jax.random.fold_in(key_of[1], 1), 0, 3).astype(jnp.int32),
        "rain_mask": draw_rain_mask(jax.random.fold_in(key_of[3], 71), 0),
    }


time_step = 0.25
wet_floor = 0.05
deep_floor = 0.1
carry_coef = 0.4
cap_floor = 0.0025
erode_coef = 0.3
settle_coef = 0.3
slide_coef = 0.1
talus_drop = 0.5
talus_sharp = 4.0
evap_coef = 0.05
rain_depth = 0.1
rock_rates = (1.0, 0.6, 0.3, 0.12)

def rock_rate(classes):
    result = rock_rates[0] * (classes == 0).astype(jnp.float32)
    for klass in range(1, 4):
        result = result + rock_rates[klass] * (classes == klass).astype(jnp.float32)
    return result

def talus_flow(diff):
    return (jax.nn.softplus(talus_sharp * (diff - talus_drop)) - jax.nn.softplus(talus_sharp * (-diff - talus_drop))) / talus_sharp

def advance(padded, erod, row_ok, col_ok):
    rows_out = padded.shape[1] - 4
    cols_out = padded.shape[2] - 4

    def inner(field, row_step, col_step):
        return field[..., 1 + row_step:3 + row_step + rows_out, 1 + col_step:3 + col_step + cols_out]

    def middle(field, row_step, col_step):
        return field[1 + row_step:1 + row_step + rows_out, 1 + col_step:1 + col_step + cols_out]

    def core(field, row_step, col_step):
        return field[..., 2 + row_step:2 + row_step + rows_out, 2 + col_step:2 + col_step + cols_out]
    height = padded[0]
    water_now = padded[1]
    surface = height + water_now
    inside = row_ok[1:3 + rows_out][:, None] * col_ok[1:3 + cols_out][None, :]
    left_ok = col_ok[0:2 + cols_out][None, :]
    right_ok = col_ok[2:4 + cols_out][None, :]
    upper_ok = row_ok[0:2 + rows_out][:, None]
    lower_ok = row_ok[2:4 + rows_out][:, None]
    centre = inner(surface, 0, 0)
    push = time_step
    to_left = jnp.maximum(0.0, inner(padded[3], 0, 0) + push * (centre - inner(surface, 0, -1))) * left_ok * inside
    to_right = jnp.maximum(0.0, inner(padded[4], 0, 0) + push * (centre - inner(surface, 0, 1))) * right_ok * inside
    to_upper = jnp.maximum(0.0, inner(padded[5], 0, 0) + push * (centre - inner(surface, -1, 0))) * upper_ok * inside
    to_lower = jnp.maximum(0.0, inner(padded[6], 0, 0) + push * (centre - inner(surface, 1, 0))) * lower_ok * inside
    raw_total = to_left + to_right + to_upper + to_lower
    limiter = jnp.minimum(1.0, inner(water_now, 0, 0) / jnp.maximum(time_step * raw_total, wet_floor))
    to_left = to_left * limiter
    to_right = to_right * limiter
    to_upper = to_upper * limiter
    to_lower = to_lower * limiter
    carried = inner(padded[2], 0, 0) / jnp.maximum(inner(water_now, 0, 0), deep_floor)
    outflow = middle(to_left, 0, 0) + middle(to_right, 0, 0) + middle(to_upper, 0, 0) + middle(to_lower, 0, 0)
    inflow = middle(to_right, 0, -1) + middle(to_left, 0, 1) + middle(to_lower, -1, 0) + middle(to_upper, 1, 0)
    water_old = core(water_now, 0, 0)
    water_new = water_old + time_step * (inflow - outflow)
    across = 0.5 * (middle(to_right, 0, -1) - middle(to_left, 0, 0) + middle(to_right, 0, 0) - middle(to_left, 0, 1))
    along = 0.5 * (middle(to_lower, -1, 0) - middle(to_upper, 0, 0) + middle(to_lower, 0, 0) - middle(to_upper, 1, 0))
    mean_depth = jnp.maximum(0.5 * (water_old + water_new), deep_floor)
    speed_u = padded[7]
    speed_v = padded[8]
    smooth_u = (4.0 * core(speed_u, 0, 0) + core(speed_u, 0, -1) + core(speed_u, 0, 1) + core(speed_u, -1, 0) + core(speed_u, 1, 0)) / 16.0
    smooth_v = (4.0 * core(speed_v, 0, 0) + core(speed_v, 0, -1) + core(speed_v, 0, 1) + core(speed_v, -1, 0) + core(speed_v, 1, 0)) / 16.0
    new_u = across / (2.0 * mean_depth) + smooth_u
    new_v = along / (2.0 * mean_depth) + smooth_v
    sediment = core(padded[2], 0, 0) + time_step * (middle(to_right, 0, -1) * middle(carried, 0, -1) + middle(to_left, 0, 1) * middle(carried, 0, 1) + middle(to_lower, -1, 0) * middle(carried, -1, 0) + middle(to_upper, 1, 0) * middle(carried, 1, 0) - outflow * middle(carried, 0, 0))
    left_in = col_ok[1:1 + cols_out][None, :]
    right_in = col_ok[3:3 + cols_out][None, :]
    upper_in = row_ok[1:1 + rows_out][:, None]
    lower_in = row_ok[3:3 + rows_out][:, None]
    base = core(height, 0, 0)
    diff_left = core(height, 0, -1) - base
    diff_right = core(height, 0, 1) - base
    diff_upper = core(height, -1, 0) - base
    diff_lower = core(height, 1, 0) - base
    grad_x = 0.5 * (right_in * diff_right - left_in * diff_left)
    grad_y = 0.5 * (lower_in * diff_lower - upper_in * diff_upper)
    grad_sq = grad_x * grad_x + grad_y * grad_y
    capacity = carry_coef * jnp.sqrt((new_u * new_u + new_v * new_v) * grad_sq / (1.0 + grad_sq) + cap_floor)
    gap_left = capacity - sediment
    delta = jnp.where(gap_left > 0.0, erode_coef * erod * gap_left, settle_coef * gap_left)
    thermal = slide_coef * (left_in * talus_flow(diff_left) + right_in * talus_flow(diff_right) + upper_in * talus_flow(diff_upper) + lower_in * talus_flow(diff_lower))
    new_height = base - delta + thermal
    new_sediment = sediment + delta
    out_ok = row_ok[2:2 + rows_out][:, None] * col_ok[2:2 + cols_out][None, :]
    fresh = jnp.stack([new_height, water_new, new_sediment, middle(to_left, 0, 0), middle(to_right, 0, 0), middle(to_upper, 0, 0), middle(to_lower, 0, 0), new_u, new_v])
    return fresh * out_ok[None]

def settle(fresh, rain_field, mean_water):
    return fresh.at[1].set(fresh[1] * (1.0 - evap_coef * mean_water) + rain_depth * rain_field)

def reference(state, hardness, rain_mask):
    row_ok = jnp.pad(jnp.ones((NX,), jnp.float32), 2)
    col_ok = jnp.pad(jnp.ones((NY,), jnp.float32), 2)
    erod = rock_rate(hardness)
    rain_field = rain_mask.astype(jnp.float32)
    for step in range(STEPS):
        padded = jnp.pad(state, ((0, 0), (2, 2), (2, 2)))
        fresh = advance(padded, erod, row_ok, col_ok)
        mean_water = jnp.sum(lax.optimization_barrier(jnp.sum(fresh[1] * fresh[1], axis=1))) / (NX * NY)
        state = settle(fresh, rain_field, mean_water)
    return state
```

```python
import jax
import jax.numpy as jnp
from jax import lax
from jax.sharding import PartitionSpec as P

STEPS = 8


time_step = 0.25
wet_floor = 0.05
deep_floor = 0.1
carry_coef = 0.4
cap_floor = 0.0025
erode_coef = 0.3
settle_coef = 0.3
slide_coef = 0.1
talus_drop = 0.5
talus_sharp = 4.0
evap_coef = 0.05
rain_depth = 0.1
rock_rates = (1.0, 0.6, 0.3, 0.12)


def with_halo(x, sides, width):
    for axis, dim in sides:
        count, length = (lax.axis_size(axis), x.shape[dim])
        up = [(i, (i + 1) % count) for i in range(count - 1)]
        down = [(j, i) for i, j in up]
        last = lax.slice_in_dim(x, length - width, length, axis=dim)
        first = lax.slice_in_dim(x, 0, width, axis=dim)
        before = lax.ppermute(last, axis, up)
        after = lax.ppermute(first, axis, down)
        x = jnp.concatenate([before, x, after], axis=dim)
    return x


def rock_rate(classes):
    result = rock_rates[0] * (classes == 0).astype(jnp.float32)
    for klass in range(1, 4):
        result = result + rock_rates[klass] * (classes == klass).astype(jnp.float32)
    return result


def talus_flow(diff):
    return (
        jax.nn.softplus(talus_sharp * (diff - talus_drop))
        - jax.nn.softplus(talus_sharp * (-diff - talus_drop))
    ) / talus_sharp


def advance(padded, erod, row_ok, col_ok):
    rows_out = padded.shape[1] - 4
    cols_out = padded.shape[2] - 4

    def inner(field, row_step, col_step):
        return field[
            ..., 1 + row_step : 3 + row_step + rows_out, 1 + col_step : 3 + col_step + cols_out
        ]

    def middle(field, row_step, col_step):
        return field[1 + row_step : 1 + row_step + rows_out, 1 + col_step : 1 + col_step + cols_out]

    def core(field, row_step, col_step):
        return field[
            ..., 2 + row_step : 2 + row_step + rows_out, 2 + col_step : 2 + col_step + cols_out
        ]

    height = padded[0]
    water_now = padded[1]
    surface = height + water_now
    inside = row_ok[1 : 3 + rows_out][:, None] * col_ok[1 : 3 + cols_out][None, :]
    left_ok = col_ok[0 : 2 + cols_out][None, :]
    right_ok = col_ok[2 : 4 + cols_out][None, :]
    upper_ok = row_ok[0 : 2 + rows_out][:, None]
    lower_ok = row_ok[2 : 4 + rows_out][:, None]
    centre = inner(surface, 0, 0)
    to_left = (
        jnp.maximum(0.0, inner(padded[3], 0, 0) + time_step * (centre - inner(surface, 0, -1)))
        * left_ok
        * inside
    )
    to_right = (
        jnp.maximum(0.0, inner(padded[4], 0, 0) + time_step * (centre - inner(surface, 0, 1)))
        * right_ok
        * inside
    )
    to_upper = (
        jnp.maximum(0.0, inner(padded[5], 0, 0) + time_step * (centre - inner(surface, -1, 0)))
        * upper_ok
        * inside
    )
    to_lower = (
        jnp.maximum(0.0, inner(padded[6], 0, 0) + time_step * (centre - inner(surface, 1, 0)))
        * lower_ok
        * inside
    )
    raw_total = to_left + to_right + to_upper + to_lower
    limiter = jnp.minimum(
        1.0, inner(water_now, 0, 0) / jnp.maximum(time_step * raw_total, wet_floor)
    )
    to_left = to_left * limiter
    to_right = to_right * limiter
    to_upper = to_upper * limiter
    to_lower = to_lower * limiter
    carried = inner(padded[2], 0, 0) / jnp.maximum(inner(water_now, 0, 0), deep_floor)
    outflow = (
        middle(to_left, 0, 0)
        + middle(to_right, 0, 0)
        + middle(to_upper, 0, 0)
        + middle(to_lower, 0, 0)
    )
    inflow = (
        middle(to_right, 0, -1)
        + middle(to_left, 0, 1)
        + middle(to_lower, -1, 0)
        + middle(to_upper, 1, 0)
    )
    water_old = core(water_now, 0, 0)
    water_new = water_old + time_step * (inflow - outflow)
    across = 0.5 * (
        middle(to_right, 0, -1)
        - middle(to_left, 0, 0)
        + middle(to_right, 0, 0)
        - middle(to_left, 0, 1)
    )
    along = 0.5 * (
        middle(to_lower, -1, 0)
        - middle(to_upper, 0, 0)
        + middle(to_lower, 0, 0)
        - middle(to_upper, 1, 0)
    )
    mean_depth = jnp.maximum(0.5 * (water_old + water_new), deep_floor)
    speed_u = padded[7]
    speed_v = padded[8]
    smooth_u = (
        4.0 * core(speed_u, 0, 0)
        + core(speed_u, 0, -1)
        + core(speed_u, 0, 1)
        + core(speed_u, -1, 0)
        + core(speed_u, 1, 0)
    ) / 16.0
    smooth_v = (
        4.0 * core(speed_v, 0, 0)
        + core(speed_v, 0, -1)
        + core(speed_v, 0, 1)
        + core(speed_v, -1, 0)
        + core(speed_v, 1, 0)
    ) / 16.0
    new_u = across / (2.0 * mean_depth) + smooth_u
    new_v = along / (2.0 * mean_depth) + smooth_v
    sediment = core(padded[2], 0, 0) + time_step * (
        middle(to_right, 0, -1) * middle(carried, 0, -1)
        + middle(to_left, 0, 1) * middle(carried, 0, 1)
        + middle(to_lower, -1, 0) * middle(carried, -1, 0)
        + middle(to_upper, 1, 0) * middle(carried, 1, 0)
        - outflow * middle(carried, 0, 0)
    )
    left_in = col_ok[1 : 1 + cols_out][None, :]
    right_in = col_ok[3 : 3 + cols_out][None, :]
    upper_in = row_ok[1 : 1 + rows_out][:, None]
    lower_in = row_ok[3 : 3 + rows_out][:, None]
    base = core(height, 0, 0)
    diff_left = core(height, 0, -1) - base
    diff_right = core(height, 0, 1) - base
    diff_upper = core(height, -1, 0) - base
    diff_lower = core(height, 1, 0) - base
    grad_x = 0.5 * (right_in * diff_right - left_in * diff_left)
    grad_y = 0.5 * (lower_in * diff_lower - upper_in * diff_upper)
    grad_sq = grad_x * grad_x + grad_y * grad_y
    capacity = carry_coef * jnp.sqrt(
        (new_u * new_u + new_v * new_v) * grad_sq / (1.0 + grad_sq) + cap_floor
    )
    gap_left = capacity - sediment
    delta = jnp.where(gap_left > 0.0, erode_coef * erod * gap_left, settle_coef * gap_left)
    thermal = slide_coef * (
        left_in * talus_flow(diff_left)
        + right_in * talus_flow(diff_right)
        + upper_in * talus_flow(diff_upper)
        + lower_in * talus_flow(diff_lower)
    )
    new_height = base - delta + thermal
    new_sediment = sediment + delta
    out_ok = row_ok[2 : 2 + rows_out][:, None] * col_ok[2 : 2 + cols_out][None, :]
    fresh = jnp.stack(
        [
            new_height,
            water_new,
            new_sediment,
            middle(to_left, 0, 0),
            middle(to_right, 0, 0),
            middle(to_upper, 0, 0),
            middle(to_lower, 0, 0),
            new_u,
            new_v,
        ]
    )
    return fresh * out_ok[None]


def settle(fresh, rain_field, mean_water):
    return fresh.at[1].set(fresh[1] * (1.0 - evap_coef * mean_water) + rain_depth * rain_field)


def valid_line(index, extent, whole, margin):
    places = index * extent + jnp.arange(-margin, extent + margin, dtype=jnp.int32)
    return ((places >= 0) & (places < whole)).astype(jnp.float32)


def butterfly_sum(value):
    total = jnp.broadcast_to(value, (1, 128))
    for axis in ("cols", "rows"):
        count = lax.axis_size(axis)
        bit = 1
        while bit < count:
            pairs = [(i, i ^ bit) for i in range(count)]
            total = total + lax.ppermute(total, axis, pairs)
            bit *= 2
    return total[0, 0]


def shards(state, hardness, rain_mask):
    rows_own = state.shape[1]
    cols_own = state.shape[2]
    whole_rows = rows_own * lax.axis_size("rows")
    whole_cols = cols_own * lax.axis_size("cols")
    cells = float(whole_rows * whole_cols)
    row_index = lax.axis_index("rows")
    col_index = lax.axis_index("cols")
    erod_own = rock_rate(hardness)
    rain_own = rain_mask.astype(jnp.float32)
    width = 2 * STEPS
    stacked = jnp.concatenate([state, erod_own[None], rain_own[None]], axis=0)
    stacked = with_halo(stacked, (("rows", 1), ("cols", 2)), width)
    current = stacked[:9]
    erod_ext = stacked[9]
    rain_ext = stacked[10]
    row_ok = valid_line(row_index, rows_own, whole_rows, width)
    col_ok = valid_line(col_index, cols_own, whole_cols, width)
    for step in range(STEPS):
        margin = width - 2 * step
        cut = 2 * step
        row_ok_now = row_ok[cut : cut + rows_own + 2 * margin]
        col_ok_now = col_ok[cut : cut + cols_own + 2 * margin]
        inner_cut = cut + 2
        out_rows = rows_own + 2 * margin - 4
        out_cols = cols_own + 2 * margin - 4
        erod_now = erod_ext[inner_cut : inner_cut + out_rows, inner_cut : inner_cut + out_cols]
        rain_now = rain_ext[inner_cut : inner_cut + out_rows, inner_cut : inner_cut + out_cols]
        fresh = advance(current, erod_now, row_ok_now, col_ok_now)
        keep = margin - 2
        own_water = fresh[1, keep : keep + rows_own, keep : keep + cols_own]
        mean_water = butterfly_sum(jnp.sum(own_water * own_water)) / cells
        current = settle(fresh, rain_now, mean_water)
    return current


def solution(mesh):
    in_specs = (P(None, "rows", "cols"), P("rows", "cols"), P("rows", "cols"))
    out_specs = P(None, "rows", "cols")
    return jax.shard_map(shards, mesh=mesh, in_specs=in_specs, out_specs=out_specs, check_vma=False)
```

```python
import jax
import jax.numpy as jnp
from jax import lax
from jax.sharding import PartitionSpec as P

STEPS = 8


time_step = 0.25
wet_floor = 0.05
deep_floor = 0.1
carry_coef = 0.4
cap_floor = 0.0025
erode_coef = 0.3
settle_coef = 0.3
slide_coef = 0.1
talus_drop = 0.5
talus_sharp = 4.0
evap_coef = 0.05
rain_depth = 0.1
rock_rates = (1.0, 0.6, 0.3, 0.12)


def with_halo(x, sides, width):
    for axis, dim in sides:
        count, length = (lax.axis_size(axis), x.shape[dim])
        up = [(i, (i + 1) % count) for i in range(count - 1)]
        down = [(j, i) for i, j in up]
        last = lax.slice_in_dim(x, length - width, length, axis=dim)
        first = lax.slice_in_dim(x, 0, width, axis=dim)
        before = lax.ppermute(last, axis, up)
        after = lax.ppermute(first, axis, down)
        x = jnp.concatenate([before, x, after], axis=dim)
    return x


def rock_rate(classes):
    result = rock_rates[0] * (classes == 0).astype(jnp.float32)
    for klass in range(1, 4):
        result = result + rock_rates[klass] * (classes == klass).astype(jnp.float32)
    return result


def talus_flow(diff):
    return (
        jax.nn.softplus(talus_sharp * (diff - talus_drop))
        - jax.nn.softplus(talus_sharp * (-diff - talus_drop))
    ) / talus_sharp


def advance(padded, erod, row_ok, col_ok):
    rows_out = padded.shape[1] - 4
    cols_out = padded.shape[2] - 4

    def inner(field, row_step, col_step):
        return field[
            ..., 1 + row_step : 3 + row_step + rows_out, 1 + col_step : 3 + col_step + cols_out
        ]

    def middle(field, row_step, col_step):
        return field[1 + row_step : 1 + row_step + rows_out, 1 + col_step : 1 + col_step + cols_out]

    def core(field, row_step, col_step):
        return field[
            ..., 2 + row_step : 2 + row_step + rows_out, 2 + col_step : 2 + col_step + cols_out
        ]

    height = padded[0]
    water_now = padded[1]
    surface = height + water_now
    inside = row_ok[1 : 3 + rows_out][:, None] * col_ok[1 : 3 + cols_out][None, :]
    left_ok = col_ok[0 : 2 + cols_out][None, :]
    right_ok = col_ok[2 : 4 + cols_out][None, :]
    upper_ok = row_ok[0 : 2 + rows_out][:, None]
    lower_ok = row_ok[2 : 4 + rows_out][:, None]
    centre = inner(surface, 0, 0)
    to_left = (
        jnp.maximum(0.0, inner(padded[3], 0, 0) + time_step * (centre - inner(surface, 0, -1)))
        * left_ok
        * inside
    )
    to_right = (
        jnp.maximum(0.0, inner(padded[4], 0, 0) + time_step * (centre - inner(surface, 0, 1)))
        * right_ok
        * inside
    )
    to_upper = (
        jnp.maximum(0.0, inner(padded[5], 0, 0) + time_step * (centre - inner(surface, -1, 0)))
        * upper_ok
        * inside
    )
    to_lower = (
        jnp.maximum(0.0, inner(padded[6], 0, 0) + time_step * (centre - inner(surface, 1, 0)))
        * lower_ok
        * inside
    )
    raw_total = to_left + to_right + to_upper + to_lower
    limiter = jnp.minimum(
        1.0, inner(water_now, 0, 0) / jnp.maximum(time_step * raw_total, wet_floor)
    )
    to_left = to_left * limiter
    to_right = to_right * limiter
    to_upper = to_upper * limiter
    to_lower = to_lower * limiter
    carried = inner(padded[2], 0, 0) / jnp.maximum(inner(water_now, 0, 0), deep_floor)
    outflow = (
        middle(to_left, 0, 0)
        + middle(to_right, 0, 0)
        + middle(to_upper, 0, 0)
        + middle(to_lower, 0, 0)
    )
    inflow = (
        middle(to_right, 0, -1)
        + middle(to_left, 0, 1)
        + middle(to_lower, -1, 0)
        + middle(to_upper, 1, 0)
    )
    water_old = core(water_now, 0, 0)
    water_new = water_old + time_step * (inflow - outflow)
    across = 0.5 * (
        middle(to_right, 0, -1)
        - middle(to_left, 0, 0)
        + middle(to_right, 0, 0)
        - middle(to_left, 0, 1)
    )
    along = 0.5 * (
        middle(to_lower, -1, 0)
        - middle(to_upper, 0, 0)
        + middle(to_lower, 0, 0)
        - middle(to_upper, 1, 0)
    )
    mean_depth = jnp.maximum(0.5 * (water_old + water_new), deep_floor)
    speed_u = padded[7]
    speed_v = padded[8]
    smooth_u = (
        4.0 * core(speed_u, 0, 0)
        + core(speed_u, 0, -1)
        + core(speed_u, 0, 1)
        + core(speed_u, -1, 0)
        + core(speed_u, 1, 0)
    ) / 16.0
    smooth_v = (
        4.0 * core(speed_v, 0, 0)
        + core(speed_v, 0, -1)
        + core(speed_v, 0, 1)
        + core(speed_v, -1, 0)
        + core(speed_v, 1, 0)
    ) / 16.0
    new_u = across / (2.0 * mean_depth) + smooth_u
    new_v = along / (2.0 * mean_depth) + smooth_v
    sediment = core(padded[2], 0, 0) + time_step * (
        middle(to_right, 0, -1) * middle(carried, 0, -1)
        + middle(to_left, 0, 1) * middle(carried, 0, 1)
        + middle(to_lower, -1, 0) * middle(carried, -1, 0)
        + middle(to_upper, 1, 0) * middle(carried, 1, 0)
        - outflow * middle(carried, 0, 0)
    )
    left_in = col_ok[1 : 1 + cols_out][None, :]
    right_in = col_ok[3 : 3 + cols_out][None, :]
    upper_in = row_ok[1 : 1 + rows_out][:, None]
    lower_in = row_ok[3 : 3 + rows_out][:, None]
    base = core(height, 0, 0)
    diff_left = core(height, 0, -1) - base
    diff_right = core(height, 0, 1) - base
    diff_upper = core(height, -1, 0) - base
    diff_lower = core(height, 1, 0) - base
    grad_x = 0.5 * (right_in * diff_right - left_in * diff_left)
    grad_y = 0.5 * (lower_in * diff_lower - upper_in * diff_upper)
    grad_sq = grad_x * grad_x + grad_y * grad_y
    capacity = carry_coef * jnp.sqrt(
        (new_u * new_u + new_v * new_v) * grad_sq / (1.0 + grad_sq) + cap_floor
    )
    gap_left = capacity - sediment
    delta = jnp.where(gap_left > 0.0, erode_coef * erod * gap_left, settle_coef * gap_left)
    thermal = slide_coef * (
        left_in * talus_flow(diff_left)
        + right_in * talus_flow(diff_right)
        + upper_in * talus_flow(diff_upper)
        + lower_in * talus_flow(diff_lower)
    )
    new_height = base - delta + thermal
    new_sediment = sediment + delta
    out_ok = row_ok[2 : 2 + rows_out][:, None] * col_ok[2 : 2 + cols_out][None, :]
    fresh = jnp.stack(
        [
            new_height,
            water_new,
            new_sediment,
            middle(to_left, 0, 0),
            middle(to_right, 0, 0),
            middle(to_upper, 0, 0),
            middle(to_lower, 0, 0),
            new_u,
            new_v,
        ]
    )
    return fresh * out_ok[None]


def settle(fresh, rain_field, mean_water):
    return fresh.at[1].set(fresh[1] * (1.0 - evap_coef * mean_water) + rain_depth * rain_field)


def valid_line(index, extent, whole, margin):
    places = index * extent + jnp.arange(-margin, extent + margin, dtype=jnp.int32)
    return ((places >= 0) & (places < whole)).astype(jnp.float32)


def flip_pairs(count, partner):
    return [(i, partner(i)) for i in range(count)]


def butterfly_sum(value):
    rows = lax.axis_size("rows")
    cols = lax.axis_size("cols")
    rounds = (
        ("cols", flip_pairs(cols, lambda c: c ^ 1)),
        ("rows", flip_pairs(rows, lambda r: r ^ 1)),
        ("rows", flip_pairs(rows, lambda r: r - r % 4 + 3 - r % 4)),
        ("rows", flip_pairs(rows, lambda r: r ^ 4)),
        ("rows", flip_pairs(rows, lambda r: r ^ 8)),
        ("rows", flip_pairs(rows, lambda r: r % 8 + 8 * (3 - r // 8))),
        ("cols", flip_pairs(cols, lambda c: c ^ 2)),
        ("cols", flip_pairs(cols, lambda c: c % 2 + 2 * (3 - c // 2))),
    )
    total = value
    for axis, pairs in rounds:
        total = total + lax.ppermute(total, axis, pairs)
    return total


def shards(state, hardness, rain_mask):
    rows_own = state.shape[1]
    cols_own = state.shape[2]
    whole_rows = rows_own * lax.axis_size("rows")
    whole_cols = cols_own * lax.axis_size("cols")
    cells = float(whole_rows * whole_cols)
    row_index = lax.axis_index("rows")
    col_index = lax.axis_index("cols")
    erod_own = rock_rate(hardness)
    rain_own = rain_mask.astype(jnp.float32)
    width = 2 * STEPS
    stacked = jnp.concatenate([state, erod_own[None], rain_own[None]], axis=0)
    stacked = with_halo(stacked, (("rows", 1), ("cols", 2)), width)
    current = stacked[:9]
    erod_ext = stacked[9]
    rain_ext = stacked[10]
    row_ok = valid_line(row_index, rows_own, whole_rows, width)
    col_ok = valid_line(col_index, cols_own, whole_cols, width)
    for step in range(STEPS):
        margin = width - 2 * step
        cut = 2 * step
        row_ok_now = row_ok[cut : cut + rows_own + 2 * margin]
        col_ok_now = col_ok[cut : cut + cols_own + 2 * margin]
        inner_cut = cut + 2
        out_rows = rows_own + 2 * margin - 4
        out_cols = cols_own + 2 * margin - 4
        erod_now = erod_ext[inner_cut : inner_cut + out_rows, inner_cut : inner_cut + out_cols]
        rain_now = rain_ext[inner_cut : inner_cut + out_rows, inner_cut : inner_cut + out_cols]
        fresh = advance(current, erod_now, row_ok_now, col_ok_now)
        keep = margin - 2
        own_water = fresh[1, keep : keep + rows_own, keep : keep + cols_own]
        mean_water = butterfly_sum(jnp.sum(own_water * own_water)) / cells
        current = settle(fresh, rain_now, mean_water)
    return current


def solution(mesh):
    in_specs = (P(None, "rows", "cols"), P("rows", "cols"), P("rows", "cols"))
    out_specs = P(None, "rows", "cols")
    return jax.shard_map(shards, mesh=mesh, in_specs=in_specs, out_specs=out_specs, check_vma=False)
```

```python
import jax
import jax.numpy as jnp
from jax import lax
from jax.sharding import PartitionSpec as P

STEPS = 8


time_step = 0.25
wet_floor = 0.05
deep_floor = 0.1
carry_coef = 0.4
cap_floor = 0.0025
erode_coef = 0.3
settle_coef = 0.3
slide_coef = 0.1
talus_drop = 0.5
talus_sharp = 4.0
evap_coef = 0.05
rain_depth = 0.1
rock_rates = (1.0, 0.6, 0.3, 0.12)


def with_halo(x, sides, width):
    for axis, dim in sides:
        count, length = (lax.axis_size(axis), x.shape[dim])
        up = [(i, (i + 1) % count) for i in range(count - 1)]
        down = [(j, i) for i, j in up]
        last = lax.slice_in_dim(x, length - width, length, axis=dim)
        first = lax.slice_in_dim(x, 0, width, axis=dim)
        before = lax.ppermute(last, axis, up)
        after = lax.ppermute(first, axis, down)
        x = jnp.concatenate([before, x, after], axis=dim)
    return x


def rock_rate(classes):
    result = rock_rates[0] * (classes == 0).astype(jnp.float32)
    for klass in range(1, 4):
        result = result + rock_rates[klass] * (classes == klass).astype(jnp.float32)
    return result


def talus_flow(diff):
    return (
        jax.nn.softplus(talus_sharp * (diff - talus_drop))
        - jax.nn.softplus(talus_sharp * (-diff - talus_drop))
    ) / talus_sharp


def advance(padded, erod, row_ok, col_ok):
    rows_out = padded.shape[1] - 4
    cols_out = padded.shape[2] - 4

    def inner(field, row_step, col_step):
        return field[
            ..., 1 + row_step : 3 + row_step + rows_out, 1 + col_step : 3 + col_step + cols_out
        ]

    def middle(field, row_step, col_step):
        return field[1 + row_step : 1 + row_step + rows_out, 1 + col_step : 1 + col_step + cols_out]

    def core(field, row_step, col_step):
        return field[
            ..., 2 + row_step : 2 + row_step + rows_out, 2 + col_step : 2 + col_step + cols_out
        ]

    height = padded[0]
    water_now = padded[1]
    surface = height + water_now
    inside = row_ok[1 : 3 + rows_out][:, None] * col_ok[1 : 3 + cols_out][None, :]
    left_ok = col_ok[0 : 2 + cols_out][None, :]
    right_ok = col_ok[2 : 4 + cols_out][None, :]
    upper_ok = row_ok[0 : 2 + rows_out][:, None]
    lower_ok = row_ok[2 : 4 + rows_out][:, None]
    centre = inner(surface, 0, 0)
    to_left = (
        jnp.maximum(0.0, inner(padded[3], 0, 0) + time_step * (centre - inner(surface, 0, -1)))
        * left_ok
        * inside
    )
    to_right = (
        jnp.maximum(0.0, inner(padded[4], 0, 0) + time_step * (centre - inner(surface, 0, 1)))
        * right_ok
        * inside
    )
    to_upper = (
        jnp.maximum(0.0, inner(padded[5], 0, 0) + time_step * (centre - inner(surface, -1, 0)))
        * upper_ok
        * inside
    )
    to_lower = (
        jnp.maximum(0.0, inner(padded[6], 0, 0) + time_step * (centre - inner(surface, 1, 0)))
        * lower_ok
        * inside
    )
    raw_total = to_left + to_right + to_upper + to_lower
    limiter = jnp.minimum(
        1.0, inner(water_now, 0, 0) / jnp.maximum(time_step * raw_total, wet_floor)
    )
    to_left = to_left * limiter
    to_right = to_right * limiter
    to_upper = to_upper * limiter
    to_lower = to_lower * limiter
    carried = inner(padded[2], 0, 0) / jnp.maximum(inner(water_now, 0, 0), deep_floor)
    outflow = (
        middle(to_left, 0, 0)
        + middle(to_right, 0, 0)
        + middle(to_upper, 0, 0)
        + middle(to_lower, 0, 0)
    )
    inflow = (
        middle(to_right, 0, -1)
        + middle(to_left, 0, 1)
        + middle(to_lower, -1, 0)
        + middle(to_upper, 1, 0)
    )
    water_old = core(water_now, 0, 0)
    water_new = water_old + time_step * (inflow - outflow)
    across = 0.5 * (
        middle(to_right, 0, -1)
        - middle(to_left, 0, 0)
        + middle(to_right, 0, 0)
        - middle(to_left, 0, 1)
    )
    along = 0.5 * (
        middle(to_lower, -1, 0)
        - middle(to_upper, 0, 0)
        + middle(to_lower, 0, 0)
        - middle(to_upper, 1, 0)
    )
    mean_depth = jnp.maximum(0.5 * (water_old + water_new), deep_floor)
    speed_u = padded[7]
    speed_v = padded[8]
    smooth_u = (
        4.0 * core(speed_u, 0, 0)
        + core(speed_u, 0, -1)
        + core(speed_u, 0, 1)
        + core(speed_u, -1, 0)
        + core(speed_u, 1, 0)
    ) / 16.0
    smooth_v = (
        4.0 * core(speed_v, 0, 0)
        + core(speed_v, 0, -1)
        + core(speed_v, 0, 1)
        + core(speed_v, -1, 0)
        + core(speed_v, 1, 0)
    ) / 16.0
    new_u = across / (2.0 * mean_depth) + smooth_u
    new_v = along / (2.0 * mean_depth) + smooth_v
    sediment = core(padded[2], 0, 0) + time_step * (
        middle(to_right, 0, -1) * middle(carried, 0, -1)
        + middle(to_left, 0, 1) * middle(carried, 0, 1)
        + middle(to_lower, -1, 0) * middle(carried, -1, 0)
        + middle(to_upper, 1, 0) * middle(carried, 1, 0)
        - outflow * middle(carried, 0, 0)
    )
    left_in = col_ok[1 : 1 + cols_out][None, :]
    right_in = col_ok[3 : 3 + cols_out][None, :]
    upper_in = row_ok[1 : 1 + rows_out][:, None]
    lower_in = row_ok[3 : 3 + rows_out][:, None]
    base = core(height, 0, 0)
    diff_left = core(height, 0, -1) - base
    diff_right = core(height, 0, 1) - base
    diff_upper = core(height, -1, 0) - base
    diff_lower = core(height, 1, 0) - base
    grad_x = 0.5 * (right_in * diff_right - left_in * diff_left)
    grad_y = 0.5 * (lower_in * diff_lower - upper_in * diff_upper)
    grad_sq = grad_x * grad_x + grad_y * grad_y
    capacity = carry_coef * jnp.sqrt(
        (new_u * new_u + new_v * new_v) * grad_sq / (1.0 + grad_sq) + cap_floor
    )
    gap_left = capacity - sediment
    delta = jnp.where(gap_left > 0.0, erode_coef * erod * gap_left, settle_coef * gap_left)
    thermal = slide_coef * (
        left_in * talus_flow(diff_left)
        + right_in * talus_flow(diff_right)
        + upper_in * talus_flow(diff_upper)
        + lower_in * talus_flow(diff_lower)
    )
    new_height = base - delta + thermal
    new_sediment = sediment + delta
    out_ok = row_ok[2 : 2 + rows_out][:, None] * col_ok[2 : 2 + cols_out][None, :]
    fresh = jnp.stack(
        [
            new_height,
            water_new,
            new_sediment,
            middle(to_left, 0, 0),
            middle(to_right, 0, 0),
            middle(to_upper, 0, 0),
            middle(to_lower, 0, 0),
            new_u,
            new_v,
        ]
    )
    return fresh * out_ok[None]


def settle(fresh, rain_field, mean_water):
    return fresh.at[1].set(fresh[1] * (1.0 - evap_coef * mean_water) + rain_depth * rain_field)


def valid_line(index, extent, whole, margin):
    places = index * extent + jnp.arange(-margin, extent + margin, dtype=jnp.int32)
    return ((places >= 0) & (places < whole)).astype(jnp.float32)


def flip_pairs(count, partner):
    return [(i, partner(i)) for i in range(count)]


def butterfly_sum(value):
    rows = lax.axis_size("rows")
    cols = lax.axis_size("cols")
    rounds = (
        ("cols", flip_pairs(cols, lambda c: c ^ 1)),
        ("rows", flip_pairs(rows, lambda r: r ^ 1)),
        ("rows", flip_pairs(rows, lambda r: r - r % 4 + 3 - r % 4)),
        ("rows", flip_pairs(rows, lambda r: r ^ 4)),
        ("rows", flip_pairs(rows, lambda r: r ^ 8)),
        ("rows", flip_pairs(rows, lambda r: r % 8 + 8 * (3 - r // 8))),
        ("cols", flip_pairs(cols, lambda c: c ^ 2)),
        ("cols", flip_pairs(cols, lambda c: c % 2 + 2 * (3 - c // 2))),
    )
    total = jnp.broadcast_to(value, (1, 128))
    for axis, pairs in rounds:
        total = total + lax.ppermute(total, axis, pairs)
    return total[0, 0]


def shards(state, hardness, rain_mask):
    rows_own = state.shape[1]
    cols_own = state.shape[2]
    whole_rows = rows_own * lax.axis_size("rows")
    whole_cols = cols_own * lax.axis_size("cols")
    cells = float(whole_rows * whole_cols)
    row_index = lax.axis_index("rows")
    col_index = lax.axis_index("cols")
    erod_own = rock_rate(hardness)
    rain_own = rain_mask.astype(jnp.float32)
    width = 2 * STEPS
    stacked = jnp.concatenate([state, erod_own[None], rain_own[None]], axis=0)
    stacked = with_halo(stacked, (("rows", 1), ("cols", 2)), width)
    current = stacked[:9]
    erod_ext = stacked[9]
    rain_ext = stacked[10]
    row_ok = valid_line(row_index, rows_own, whole_rows, width)
    col_ok = valid_line(col_index, cols_own, whole_cols, width)
    for step in range(STEPS):
        margin = width - 2 * step
        cut = 2 * step
        row_ok_now = row_ok[cut : cut + rows_own + 2 * margin]
        col_ok_now = col_ok[cut : cut + cols_own + 2 * margin]
        inner_cut = cut + 2
        out_rows = rows_own + 2 * margin - 4
        out_cols = cols_own + 2 * margin - 4
        erod_now = erod_ext[inner_cut : inner_cut + out_rows, inner_cut : inner_cut + out_cols]
        rain_now = rain_ext[inner_cut : inner_cut + out_rows, inner_cut : inner_cut + out_cols]
        fresh = advance(current, erod_now, row_ok_now, col_ok_now)
        keep = margin - 2
        own_water = fresh[1, keep : keep + rows_own, keep : keep + cols_own]
        mean_water = butterfly_sum(jnp.sum(own_water * own_water)) / cells
        current = settle(fresh, rain_now, mean_water)
    return current


def solution(mesh):
    in_specs = (P(None, "rows", "cols"), P("rows", "cols"), P("rows", "cols"))
    out_specs = P(None, "rows", "cols")
    return jax.shard_map(shards, mesh=mesh, in_specs=in_specs, out_specs=out_specs, check_vma=False)
```

```python
import jax
import jax.numpy as jnp
from jax import lax
from jax.sharding import PartitionSpec as P

STEPS = 8


time_step = 0.25
wet_floor = 0.05
deep_floor = 0.1
carry_coef = 0.4
cap_floor = 0.0025
erode_coef = 0.3
settle_coef = 0.3
slide_coef = 0.1
talus_drop = 0.5
talus_sharp = 4.0
evap_coef = 0.05
rain_depth = 0.1
rock_rates = (1.0, 0.6, 0.3, 0.12)


def with_halo(x, width):
    rows = lax.axis_size("rows")
    cols = lax.axis_size("cols")
    length_r, length_c = x.shape[1], x.shape[2]
    pick = {-1: (length_r - width, length_r), 0: (0, length_r), 1: (0, width)}
    pick_c = {-1: (length_c - width, length_c), 0: (0, length_c), 1: (0, width)}
    parts = {}
    for dr in (-1, 0, 1):
        for dc in (-1, 0, 1):
            if dr == 0 and dc == 0:
                parts[(dr, dc)] = x
                continue
            pairs = []
            for r in range(rows):
                for c in range(cols):
                    sr, sc = r + dr, c + dc
                    if 0 <= sr < rows and 0 <= sc < cols:
                        pairs.append((sr * cols + sc, r * cols + c))
            r0, r1 = pick[dr]
            c0, c1 = pick_c[dc]
            piece = x[:, r0:r1, c0:c1]
            parts[(dr, dc)] = lax.ppermute(piece, ("rows", "cols"), pairs)
    bands = [jnp.concatenate([parts[(dr, -1)], parts[(dr, 0)], parts[(dr, 1)]], axis=2) for dr in (-1, 0, 1)]
    return jnp.concatenate(bands, axis=1)


def rock_rate(classes):
    result = rock_rates[0] * (classes == 0).astype(jnp.float32)
    for klass in range(1, 4):
        result = result + rock_rates[klass] * (classes == klass).astype(jnp.float32)
    return result


def talus_flow(diff):
    return (
        jax.nn.softplus(talus_sharp * (diff - talus_drop))
        - jax.nn.softplus(talus_sharp * (-diff - talus_drop))
    ) / talus_sharp


def advance(padded, erod, row_ok, col_ok):
    rows_out = padded.shape[1] - 4
    cols_out = padded.shape[2] - 4

    def inner(field, row_step, col_step):
        return field[
            ..., 1 + row_step : 3 + row_step + rows_out, 1 + col_step : 3 + col_step + cols_out
        ]

    def middle(field, row_step, col_step):
        return field[1 + row_step : 1 + row_step + rows_out, 1 + col_step : 1 + col_step + cols_out]

    def core(field, row_step, col_step):
        return field[
            ..., 2 + row_step : 2 + row_step + rows_out, 2 + col_step : 2 + col_step + cols_out
        ]

    height = padded[0]
    water_now = padded[1]
    surface = height + water_now
    inside = row_ok[1 : 3 + rows_out][:, None] * col_ok[1 : 3 + cols_out][None, :]
    left_ok = col_ok[0 : 2 + cols_out][None, :]
    right_ok = col_ok[2 : 4 + cols_out][None, :]
    upper_ok = row_ok[0 : 2 + rows_out][:, None]
    lower_ok = row_ok[2 : 4 + rows_out][:, None]
    centre = inner(surface, 0, 0)
    to_left = (
        jnp.maximum(0.0, inner(padded[3], 0, 0) + time_step * (centre - inner(surface, 0, -1)))
        * left_ok
        * inside
    )
    to_right = (
        jnp.maximum(0.0, inner(padded[4], 0, 0) + time_step * (centre - inner(surface, 0, 1)))
        * right_ok
        * inside
    )
    to_upper = (
        jnp.maximum(0.0, inner(padded[5], 0, 0) + time_step * (centre - inner(surface, -1, 0)))
        * upper_ok
        * inside
    )
    to_lower = (
        jnp.maximum(0.0, inner(padded[6], 0, 0) + time_step * (centre - inner(surface, 1, 0)))
        * lower_ok
        * inside
    )
    raw_total = to_left + to_right + to_upper + to_lower
    limiter = jnp.minimum(
        1.0, inner(water_now, 0, 0) / jnp.maximum(time_step * raw_total, wet_floor)
    )
    to_left = to_left * limiter
    to_right = to_right * limiter
    to_upper = to_upper * limiter
    to_lower = to_lower * limiter
    carried = inner(padded[2], 0, 0) / jnp.maximum(inner(water_now, 0, 0), deep_floor)
    outflow = (
        middle(to_left, 0, 0)
        + middle(to_right, 0, 0)
        + middle(to_upper, 0, 0)
        + middle(to_lower, 0, 0)
    )
    inflow = (
        middle(to_right, 0, -1)
        + middle(to_left, 0, 1)
        + middle(to_lower, -1, 0)
        + middle(to_upper, 1, 0)
    )
    water_old = core(water_now, 0, 0)
    water_new = water_old + time_step * (inflow - outflow)
    to_left, to_right, to_upper, to_lower, water_new = lax.optimization_barrier(
        (to_left, to_right, to_upper, to_lower, water_new)
    )
    across = 0.5 * (
        middle(to_right, 0, -1)
        - middle(to_left, 0, 0)
        + middle(to_right, 0, 0)
        - middle(to_left, 0, 1)
    )
    along = 0.5 * (
        middle(to_lower, -1, 0)
        - middle(to_upper, 0, 0)
        + middle(to_lower, 0, 0)
        - middle(to_upper, 1, 0)
    )
    mean_depth = jnp.maximum(0.5 * (water_old + water_new), deep_floor)
    speed_u = padded[7]
    speed_v = padded[8]
    smooth_u = (
        4.0 * core(speed_u, 0, 0)
        + core(speed_u, 0, -1)
        + core(speed_u, 0, 1)
        + core(speed_u, -1, 0)
        + core(speed_u, 1, 0)
    ) / 16.0
    smooth_v = (
        4.0 * core(speed_v, 0, 0)
        + core(speed_v, 0, -1)
        + core(speed_v, 0, 1)
        + core(speed_v, -1, 0)
        + core(speed_v, 1, 0)
    ) / 16.0
    new_u = across / (2.0 * mean_depth) + smooth_u
    new_v = along / (2.0 * mean_depth) + smooth_v
    sediment = core(padded[2], 0, 0) + time_step * (
        middle(to_right, 0, -1) * middle(carried, 0, -1)
        + middle(to_left, 0, 1) * middle(carried, 0, 1)
        + middle(to_lower, -1, 0) * middle(carried, -1, 0)
        + middle(to_upper, 1, 0) * middle(carried, 1, 0)
        - outflow * middle(carried, 0, 0)
    )
    left_in = col_ok[1 : 1 + cols_out][None, :]
    right_in = col_ok[3 : 3 + cols_out][None, :]
    upper_in = row_ok[1 : 1 + rows_out][:, None]
    lower_in = row_ok[3 : 3 + rows_out][:, None]
    base = core(height, 0, 0)
    diff_left = core(height, 0, -1) - base
    diff_right = core(height, 0, 1) - base
    diff_upper = core(height, -1, 0) - base
    diff_lower = core(height, 1, 0) - base
    grad_x = 0.5 * (right_in * diff_right - left_in * diff_left)
    grad_y = 0.5 * (lower_in * diff_lower - upper_in * diff_upper)
    grad_sq = grad_x * grad_x + grad_y * grad_y
    capacity = carry_coef * jnp.sqrt(
        (new_u * new_u + new_v * new_v) * grad_sq / (1.0 + grad_sq) + cap_floor
    )
    gap_left = capacity - sediment
    delta = jnp.where(gap_left > 0.0, erode_coef * erod * gap_left, settle_coef * gap_left)
    thermal = slide_coef * (
        left_in * talus_flow(diff_left)
        + right_in * talus_flow(diff_right)
        + upper_in * talus_flow(diff_upper)
        + lower_in * talus_flow(diff_lower)
    )
    new_height = base - delta + thermal
    new_sediment = sediment + delta
    out_ok = row_ok[2 : 2 + rows_out][:, None] * col_ok[2 : 2 + cols_out][None, :]
    fresh = jnp.stack(
        [
            new_height,
            water_new,
            new_sediment,
            middle(to_left, 0, 0),
            middle(to_right, 0, 0),
            middle(to_upper, 0, 0),
            middle(to_lower, 0, 0),
            new_u,
            new_v,
        ]
    )
    return fresh * out_ok[None], water_new


def settle(fresh, rain_field, mean_water):
    return fresh.at[1].set(fresh[1] * (1.0 - evap_coef * mean_water) + rain_depth * rain_field)


def valid_line(index, extent, whole, margin):
    places = index * extent + jnp.arange(-margin, extent + margin, dtype=jnp.int32)
    return ((places >= 0) & (places < whole)).astype(jnp.float32)


def flip_pairs(count, partner):
    return [(i, partner(i)) for i in range(count)]


def butterfly_sum(value):
    rows = lax.axis_size("rows")
    cols = lax.axis_size("cols")
    rounds = (
        ("cols", flip_pairs(cols, lambda c: c ^ 1)),
        ("rows", flip_pairs(rows, lambda r: r ^ 1)),
        ("rows", flip_pairs(rows, lambda r: r - r % 4 + 3 - r % 4)),
        ("rows", flip_pairs(rows, lambda r: r ^ 4)),
        ("rows", flip_pairs(rows, lambda r: r ^ 8)),
        ("rows", flip_pairs(rows, lambda r: r % 8 + 8 * (3 - r // 8))),
        ("cols", flip_pairs(cols, lambda c: c ^ 2)),
        ("cols", flip_pairs(cols, lambda c: c % 2 + 2 * (3 - c // 2))),
    )
    total = jnp.broadcast_to(value, (1, 128))
    for axis, pairs in rounds:
        total = total + lax.ppermute(total, axis, pairs)
    return total[0, 0]


def shards(state, hardness, rain_mask):
    rows_own = state.shape[1]
    cols_own = state.shape[2]
    whole_rows = rows_own * lax.axis_size("rows")
    whole_cols = cols_own * lax.axis_size("cols")
    cells = float(whole_rows * whole_cols)
    row_index = lax.axis_index("rows")
    col_index = lax.axis_index("cols")
    erod_own = rock_rate(hardness)
    rain_own = rain_mask.astype(jnp.float32)
    width = 2 * STEPS
    stacked = jnp.concatenate([state, erod_own[None], rain_own[None]], axis=0)
    stacked = with_halo(stacked, width)
    current = stacked[:9]
    erod_ext = stacked[9]
    rain_ext = stacked[10]
    row_ok = valid_line(row_index, rows_own, whole_rows, width)
    col_ok = valid_line(col_index, cols_own, whole_cols, width)
    for step in range(STEPS):
        margin = width - 2 * step
        cut = 2 * step
        row_ok_now = row_ok[cut : cut + rows_own + 2 * margin]
        col_ok_now = col_ok[cut : cut + cols_own + 2 * margin]
        inner_cut = cut + 2
        out_rows = rows_own + 2 * margin - 4
        out_cols = cols_own + 2 * margin - 4
        erod_now = erod_ext[inner_cut : inner_cut + out_rows, inner_cut : inner_cut + out_cols]
        rain_now = rain_ext[inner_cut : inner_cut + out_rows, inner_cut : inner_cut + out_cols]
        fresh, water_new = advance(current, erod_now, row_ok_now, col_ok_now)
        keep = margin - 2
        own_water = water_new[keep : keep + rows_own, keep : keep + cols_own]
        mean_water = butterfly_sum(jnp.sum(own_water * own_water)) / cells
        current = settle(fresh, rain_now, mean_water)
    return current


def solution(mesh):
    in_specs = (P(None, "rows", "cols"), P("rows", "cols"), P("rows", "cols"))
    out_specs = P(None, "rows", "cols")
    return jax.shard_map(shards, mesh=mesh, in_specs=in_specs, out_specs=out_specs, check_vma=False)
```

```python
import jax
import jax.numpy as jnp
from jax import lax
from jax.sharding import PartitionSpec as P

STEPS = 8


time_step = 0.25
wet_floor = 0.05
deep_floor = 0.1
carry_coef = 0.4
cap_floor = 0.0025
erode_coef = 0.3
settle_coef = 0.3
slide_coef = 0.1
talus_drop = 0.5
talus_sharp = 4.0
evap_coef = 0.05
rain_depth = 0.1
rock_rates = (1.0, 0.6, 0.3, 0.12)


def with_halo(x, sides, width):
    for axis, dim in sides:
        count, length = (lax.axis_size(axis), x.shape[dim])
        up = [(i, (i + 1) % count) for i in range(count - 1)]
        down = [(j, i) for i, j in up]
        last = lax.slice_in_dim(x, length - width, length, axis=dim)
        first = lax.slice_in_dim(x, 0, width, axis=dim)
        before = lax.ppermute(last, axis, up)
        after = lax.ppermute(first, axis, down)
        x = jnp.concatenate([before, x, after], axis=dim)
    return x


def rock_rate(classes):
    result = rock_rates[0] * (classes == 0).astype(jnp.float32)
    for klass in range(1, 4):
        result = result + rock_rates[klass] * (classes == klass).astype(jnp.float32)
    return result


def talus_flow(diff):
    return (
        jax.nn.softplus(talus_sharp * (diff - talus_drop))
        - jax.nn.softplus(talus_sharp * (-diff - talus_drop))
    ) / talus_sharp


def advance(padded, erod, row_ok, col_ok):
    rows_out = padded.shape[1] - 4
    cols_out = padded.shape[2] - 4

    def inner(field, row_step, col_step):
        return field[
            ..., 1 + row_step : 3 + row_step + rows_out, 1 + col_step : 3 + col_step + cols_out
        ]

    def middle(field, row_step, col_step):
        return field[1 + row_step : 1 + row_step + rows_out, 1 + col_step : 1 + col_step + cols_out]

    def core(field, row_step, col_step):
        return field[
            ..., 2 + row_step : 2 + row_step + rows_out, 2 + col_step : 2 + col_step + cols_out
        ]

    height = padded[0]
    water_now = padded[1]
    surface = height + water_now
    inside = row_ok[1 : 3 + rows_out][:, None] * col_ok[1 : 3 + cols_out][None, :]
    left_ok = col_ok[0 : 2 + cols_out][None, :]
    right_ok = col_ok[2 : 4 + cols_out][None, :]
    upper_ok = row_ok[0 : 2 + rows_out][:, None]
    lower_ok = row_ok[2 : 4 + rows_out][:, None]
    centre = inner(surface, 0, 0)
    to_left = (
        jnp.maximum(0.0, inner(padded[3], 0, 0) + time_step * (centre - inner(surface, 0, -1)))
        * left_ok
        * inside
    )
    to_right = (
        jnp.maximum(0.0, inner(padded[4], 0, 0) + time_step * (centre - inner(surface, 0, 1)))
        * right_ok
        * inside
    )
    to_upper = (
        jnp.maximum(0.0, inner(padded[5], 0, 0) + time_step * (centre - inner(surface, -1, 0)))
        * upper_ok
        * inside
    )
    to_lower = (
        jnp.maximum(0.0, inner(padded[6], 0, 0) + time_step * (centre - inner(surface, 1, 0)))
        * lower_ok
        * inside
    )
    raw_total = to_left + to_right + to_upper + to_lower
    limiter = jnp.minimum(
        1.0, inner(water_now, 0, 0) / jnp.maximum(time_step * raw_total, wet_floor)
    )
    to_left = to_left * limiter
    to_right = to_right * limiter
    to_upper = to_upper * limiter
    to_lower = to_lower * limiter
    carried = inner(padded[2], 0, 0) / jnp.maximum(inner(water_now, 0, 0), deep_floor)
    outflow = (
        middle(to_left, 0, 0)
        + middle(to_right, 0, 0)
        + middle(to_upper, 0, 0)
        + middle(to_lower, 0, 0)
    )
    inflow = (
        middle(to_right, 0, -1)
        + middle(to_left, 0, 1)
        + middle(to_lower, -1, 0)
        + middle(to_upper, 1, 0)
    )
    water_old = core(water_now, 0, 0)
    water_new = water_old + time_step * (inflow - outflow)
    to_left, to_right, to_upper, to_lower, water_new = lax.optimization_barrier(
        (to_left, to_right, to_upper, to_lower, water_new)
    )
    across = 0.5 * (
        middle(to_right, 0, -1)
        - middle(to_left, 0, 0)
        + middle(to_right, 0, 0)
        - middle(to_left, 0, 1)
    )
    along = 0.5 * (
        middle(to_lower, -1, 0)
        - middle(to_upper, 0, 0)
        + middle(to_lower, 0, 0)
        - middle(to_upper, 1, 0)
    )
    mean_depth = jnp.maximum(0.5 * (water_old + water_new), deep_floor)
    speed_u = padded[7]
    speed_v = padded[8]
    smooth_u = (
        4.0 * core(speed_u, 0, 0)
        + core(speed_u, 0, -1)
        + core(speed_u, 0, 1)
        + core(speed_u, -1, 0)
        + core(speed_u, 1, 0)
    ) / 16.0
    smooth_v = (
        4.0 * core(speed_v, 0, 0)
        + core(speed_v, 0, -1)
        + core(speed_v, 0, 1)
        + core(speed_v, -1, 0)
        + core(speed_v, 1, 0)
    ) / 16.0
    new_u = across / (2.0 * mean_depth) + smooth_u
    new_v = along / (2.0 * mean_depth) + smooth_v
    sediment = core(padded[2], 0, 0) + time_step * (
        middle(to_right, 0, -1) * middle(carried, 0, -1)
        + middle(to_left, 0, 1) * middle(carried, 0, 1)
        + middle(to_lower, -1, 0) * middle(carried, -1, 0)
        + middle(to_upper, 1, 0) * middle(carried, 1, 0)
        - outflow * middle(carried, 0, 0)
    )
    left_in = col_ok[1 : 1 + cols_out][None, :]
    right_in = col_ok[3 : 3 + cols_out][None, :]
    upper_in = row_ok[1 : 1 + rows_out][:, None]
    lower_in = row_ok[3 : 3 + rows_out][:, None]
    base = core(height, 0, 0)
    diff_left = core(height, 0, -1) - base
    diff_right = core(height, 0, 1) - base
    diff_upper = core(height, -1, 0) - base
    diff_lower = core(height, 1, 0) - base
    grad_x = 0.5 * (right_in * diff_right - left_in * diff_left)
    grad_y = 0.5 * (lower_in * diff_lower - upper_in * diff_upper)
    grad_sq = grad_x * grad_x + grad_y * grad_y
    capacity = carry_coef * jnp.sqrt(
        (new_u * new_u + new_v * new_v) * grad_sq / (1.0 + grad_sq) + cap_floor
    )
    gap_left = capacity - sediment
    delta = jnp.where(gap_left > 0.0, erode_coef * erod * gap_left, settle_coef * gap_left)
    thermal = slide_coef * (
        left_in * talus_flow(diff_left)
        + right_in * talus_flow(diff_right)
        + upper_in * talus_flow(diff_upper)
        + lower_in * talus_flow(diff_lower)
    )
    new_height = base - delta + thermal
    new_sediment = sediment + delta
    out_ok = row_ok[2 : 2 + rows_out][:, None] * col_ok[2 : 2 + cols_out][None, :]
    fresh = jnp.stack(
        [
            new_height,
            water_new,
            new_sediment,
            middle(to_left, 0, 0),
            middle(to_right, 0, 0),
            middle(to_upper, 0, 0),
            middle(to_lower, 0, 0),
            new_u,
            new_v,
        ]
    )
    return fresh * out_ok[None], water_new


def settle(fresh, rain_field, mean_water):
    return fresh.at[1].set(fresh[1] * (1.0 - evap_coef * mean_water) + rain_depth * rain_field)


def valid_line(index, extent, whole, margin):
    places = index * extent + jnp.arange(-margin, extent + margin, dtype=jnp.int32)
    return ((places >= 0) & (places < whole)).astype(jnp.float32)


def flip_pairs(count, partner):
    return [(i, partner(i)) for i in range(count)]


def butterfly_sum(value):
    rows = lax.axis_size("rows")
    cols = lax.axis_size("cols")
    rounds = (
        ("cols", flip_pairs(cols, lambda c: c ^ 1)),
        ("rows", flip_pairs(rows, lambda r: r ^ 1)),
        ("rows", flip_pairs(rows, lambda r: r - r % 4 + 3 - r % 4)),
        ("rows", flip_pairs(rows, lambda r: r ^ 4)),
        ("rows", flip_pairs(rows, lambda r: r ^ 8)),
        ("rows", flip_pairs(rows, lambda r: r % 8 + 8 * (3 - r // 8))),
        ("cols", flip_pairs(cols, lambda c: c ^ 2)),
        ("cols", flip_pairs(cols, lambda c: c % 2 + 2 * (3 - c // 2))),
    )
    total = value
    for axis, pairs in rounds:
        total = total + lax.ppermute(total, axis, pairs)
    return jnp.sum(total)


def shards(state, hardness, rain_mask):
    rows_own = state.shape[1]
    cols_own = state.shape[2]
    whole_rows = rows_own * lax.axis_size("rows")
    whole_cols = cols_own * lax.axis_size("cols")
    cells = float(whole_rows * whole_cols)
    row_index = lax.axis_index("rows")
    col_index = lax.axis_index("cols")
    erod_own = rock_rate(hardness)
    rain_own = rain_mask.astype(jnp.float32)
    width = 2 * STEPS
    stacked = jnp.concatenate([state, erod_own[None], rain_own[None]], axis=0)
    stacked = with_halo(stacked, (("rows", 1), ("cols", 2)), width)
    current = stacked[:9]
    erod_ext = stacked[9]
    rain_ext = stacked[10]
    row_ok = valid_line(row_index, rows_own, whole_rows, width)
    col_ok = valid_line(col_index, cols_own, whole_cols, width)
    for step in range(STEPS):
        margin = width - 2 * step
        cut = 2 * step
        row_ok_now = row_ok[cut : cut + rows_own + 2 * margin]
        col_ok_now = col_ok[cut : cut + cols_own + 2 * margin]
        inner_cut = cut + 2
        out_rows = rows_own + 2 * margin - 4
        out_cols = cols_own + 2 * margin - 4
        erod_now = erod_ext[inner_cut : inner_cut + out_rows, inner_cut : inner_cut + out_cols]
        rain_now = rain_ext[inner_cut : inner_cut + out_rows, inner_cut : inner_cut + out_cols]
        fresh, water_new = advance(current, erod_now, row_ok_now, col_ok_now)
        keep = margin - 2
        own_water = water_new[keep : keep + rows_own, keep : keep + cols_own]
        lanes = jnp.sum(jnp.reshape(own_water * own_water, (-1, 128)), axis=0, keepdims=True)
        mean_water = butterfly_sum(lanes) / cells
        current = settle(fresh, rain_now, mean_water)
    return current


def solution(mesh):
    in_specs = (P(None, "rows", "cols"), P("rows", "cols"), P("rows", "cols"))
    out_specs = P(None, "rows", "cols")
    return jax.shard_map(shards, mesh=mesh, in_specs=in_specs, out_specs=out_specs, check_vma=False)
```

```python
import jax
import jax.numpy as jnp
from jax import lax
from jax.sharding import PartitionSpec as P

STEPS = 8


time_step = 0.25
wet_floor = 0.05
deep_floor = 0.1
carry_coef = 0.4
cap_floor = 0.0025
erode_coef = 0.3
settle_coef = 0.3
slide_coef = 0.1
talus_drop = 0.5
talus_sharp = 4.0
evap_coef = 0.05
rain_depth = 0.1
rock_rates = (1.0, 0.6, 0.3, 0.12)


def with_halo(x, sides, width):
    for axis, dim in sides:
        count, length = (lax.axis_size(axis), x.shape[dim])
        up = [(i, (i + 1) % count) for i in range(count - 1)]
        down = [(j, i) for i, j in up]
        last = lax.slice_in_dim(x, length - width, length, axis=dim)
        first = lax.slice_in_dim(x, 0, width, axis=dim)
        before = lax.ppermute(last, axis, up)
        after = lax.ppermute(first, axis, down)
        x = jnp.concatenate([before, x, after], axis=dim)
    return x


def rock_rate(classes):
    result = rock_rates[0] * (classes == 0).astype(jnp.float32)
    for klass in range(1, 4):
        result = result + rock_rates[klass] * (classes == klass).astype(jnp.float32)
    return result


def talus_flow(diff):
    return (
        jax.nn.softplus(talus_sharp * (diff - talus_drop))
        - jax.nn.softplus(talus_sharp * (-diff - talus_drop))
    ) / talus_sharp


def advance(padded, erod, row_ok, col_ok):
    rows_out = padded.shape[1] - 4
    cols_out = padded.shape[2] - 4

    def inner(field, row_step, col_step):
        return field[
            ..., 1 + row_step : 3 + row_step + rows_out, 1 + col_step : 3 + col_step + cols_out
        ]

    def middle(field, row_step, col_step):
        return field[1 + row_step : 1 + row_step + rows_out, 1 + col_step : 1 + col_step + cols_out]

    def core(field, row_step, col_step):
        return field[
            ..., 2 + row_step : 2 + row_step + rows_out, 2 + col_step : 2 + col_step + cols_out
        ]

    height = padded[0]
    water_now = padded[1]
    surface = height + water_now
    inside = row_ok[1 : 3 + rows_out][:, None] * col_ok[1 : 3 + cols_out][None, :]
    left_ok = col_ok[0 : 2 + cols_out][None, :]
    right_ok = col_ok[2 : 4 + cols_out][None, :]
    upper_ok = row_ok[0 : 2 + rows_out][:, None]
    lower_ok = row_ok[2 : 4 + rows_out][:, None]
    centre = inner(surface, 0, 0)
    to_left = (
        jnp.maximum(0.0, inner(padded[3], 0, 0) + time_step * (centre - inner(surface, 0, -1)))
        * left_ok
        * inside
    )
    to_right = (
        jnp.maximum(0.0, inner(padded[4], 0, 0) + time_step * (centre - inner(surface, 0, 1)))
        * right_ok
        * inside
    )
    to_upper = (
        jnp.maximum(0.0, inner(padded[5], 0, 0) + time_step * (centre - inner(surface, -1, 0)))
        * upper_ok
        * inside
    )
    to_lower = (
        jnp.maximum(0.0, inner(padded[6], 0, 0) + time_step * (centre - inner(surface, 1, 0)))
        * lower_ok
        * inside
    )
    raw_total = to_left + to_right + to_upper + to_lower
    limiter = jnp.minimum(
        1.0, inner(water_now, 0, 0) / jnp.maximum(time_step * raw_total, wet_floor)
    )
    to_left = to_left * limiter
    to_right = to_right * limiter
    to_upper = to_upper * limiter
    to_lower = to_lower * limiter
    carried = inner(padded[2], 0, 0) / jnp.maximum(inner(water_now, 0, 0), deep_floor)
    outflow = (
        middle(to_left, 0, 0)
        + middle(to_right, 0, 0)
        + middle(to_upper, 0, 0)
        + middle(to_lower, 0, 0)
    )
    inflow = (
        middle(to_right, 0, -1)
        + middle(to_left, 0, 1)
        + middle(to_lower, -1, 0)
        + middle(to_upper, 1, 0)
    )
    water_old = core(water_now, 0, 0)
    water_new = water_old + time_step * (inflow - outflow)
    to_left, to_right, to_upper, to_lower, water_new = lax.optimization_barrier(
        (to_left, to_right, to_upper, to_lower, water_new)
    )
    across = 0.5 * (
        middle(to_right, 0, -1)
        - middle(to_left, 0, 0)
        + middle(to_right, 0, 0)
        - middle(to_left, 0, 1)
    )
    along = 0.5 * (
        middle(to_lower, -1, 0)
        - middle(to_upper, 0, 0)
        + middle(to_lower, 0, 0)
        - middle(to_upper, 1, 0)
    )
    mean_depth = jnp.maximum(0.5 * (water_old + water_new), deep_floor)
    speed_u = padded[7]
    speed_v = padded[8]
    smooth_u = (
        4.0 * core(speed_u, 0, 0)
        + core(speed_u, 0, -1)
        + core(speed_u, 0, 1)
        + core(speed_u, -1, 0)
        + core(speed_u, 1, 0)
    ) / 16.0
    smooth_v = (
        4.0 * core(speed_v, 0, 0)
        + core(speed_v, 0, -1)
        + core(speed_v, 0, 1)
        + core(speed_v, -1, 0)
        + core(speed_v, 1, 0)
    ) / 16.0
    new_u = across / (2.0 * mean_depth) + smooth_u
    new_v = along / (2.0 * mean_depth) + smooth_v
    sediment = core(padded[2], 0, 0) + time_step * (
        middle(to_right, 0, -1) * middle(carried, 0, -1)
        + middle(to_left, 0, 1) * middle(carried, 0, 1)
        + middle(to_lower, -1, 0) * middle(carried, -1, 0)
        + middle(to_upper, 1, 0) * middle(carried, 1, 0)
        - outflow * middle(carried, 0, 0)
    )
    left_in = col_ok[1 : 1 + cols_out][None, :]
    right_in = col_ok[3 : 3 + cols_out][None, :]
    upper_in = row_ok[1 : 1 + rows_out][:, None]
    lower_in = row_ok[3 : 3 + rows_out][:, None]
    base = core(height, 0, 0)
    diff_left = core(height, 0, -1) - base
    diff_right = core(height, 0, 1) - base
    diff_upper = core(height, -1, 0) - base
    diff_lower = core(height, 1, 0) - base
    grad_x = 0.5 * (right_in * diff_right - left_in * diff_left)
    grad_y = 0.5 * (lower_in * diff_lower - upper_in * diff_upper)
    grad_sq = grad_x * grad_x + grad_y * grad_y
    capacity = carry_coef * jnp.sqrt(
        (new_u * new_u + new_v * new_v) * grad_sq / (1.0 + grad_sq) + cap_floor
    )
    gap_left = capacity - sediment
    delta = jnp.where(gap_left > 0.0, erode_coef * erod * gap_left, settle_coef * gap_left)
    thermal = slide_coef * (
        left_in * talus_flow(diff_left)
        + right_in * talus_flow(diff_right)
        + upper_in * talus_flow(diff_upper)
        + lower_in * talus_flow(diff_lower)
    )
    new_height = base - delta + thermal
    new_sediment = sediment + delta
    out_ok = row_ok[2 : 2 + rows_out][:, None] * col_ok[2 : 2 + cols_out][None, :]
    fresh = jnp.stack(
        [
            new_height,
            water_new,
            new_sediment,
            middle(to_left, 0, 0),
            middle(to_right, 0, 0),
            middle(to_upper, 0, 0),
            middle(to_lower, 0, 0),
            new_u,
            new_v,
        ]
    )
    return fresh * out_ok[None], water_new


def settle(fresh, rain_field, mean_water):
    return fresh.at[1].set(fresh[1] * (1.0 - evap_coef * mean_water) + rain_depth * rain_field)


def valid_line(index, extent, whole, margin):
    places = index * extent + jnp.arange(-margin, extent + margin, dtype=jnp.int32)
    return ((places >= 0) & (places < whole)).astype(jnp.float32)


def flip_pairs(count, partner):
    return [(i, partner(i)) for i in range(count)]


def butterfly_sum(value):
    rows = lax.axis_size("rows")
    cols = lax.axis_size("cols")
    rounds = (
        ("cols", flip_pairs(cols, lambda c: c ^ 1)),
        ("rows", flip_pairs(rows, lambda r: r ^ 1)),
        ("rows", flip_pairs(rows, lambda r: r - r % 4 + 3 - r % 4)),
        ("rows", flip_pairs(rows, lambda r: r ^ 4)),
        ("rows", flip_pairs(rows, lambda r: r ^ 8)),
        ("rows", flip_pairs(rows, lambda r: r % 8 + 8 * (3 - r // 8))),
        ("cols", flip_pairs(cols, lambda c: c ^ 2)),
        ("cols", flip_pairs(cols, lambda c: c % 2 + 2 * (3 - c // 2))),
    )
    total = jnp.broadcast_to(value, (1, 128))
    for axis, pairs in rounds:
        total = total + lax.ppermute(total, axis, pairs)
    return total[0, 0]


def shards(state, hardness, rain_mask):
    rows_own = state.shape[1]
    cols_own = state.shape[2]
    whole_rows = rows_own * lax.axis_size("rows")
    whole_cols = cols_own * lax.axis_size("cols")
    cells = float(whole_rows * whole_cols)
    row_index = lax.axis_index("rows")
    col_index = lax.axis_index("cols")
    erod_own = rock_rate(hardness)
    rain_own = rain_mask.astype(jnp.float32)
    width = 2 * STEPS
    stacked = jnp.concatenate([state, erod_own[None], rain_own[None]], axis=0)
    stacked = with_halo(stacked, (("rows", 1), ("cols", 2)), width)
    current = stacked[:9]
    erod_ext = stacked[9]
    rain_ext = stacked[10]
    row_ok = valid_line(row_index, rows_own, whole_rows, width)
    col_ok = valid_line(col_index, cols_own, whole_cols, width)
    for step in range(STEPS):
        margin = width - 2 * step
        cut = 2 * step
        row_ok_now = row_ok[cut : cut + rows_own + 2 * margin]
        col_ok_now = col_ok[cut : cut + cols_own + 2 * margin]
        inner_cut = cut + 2
        out_rows = rows_own + 2 * margin - 4
        out_cols = cols_own + 2 * margin - 4
        erod_now = erod_ext[inner_cut : inner_cut + out_rows, inner_cut : inner_cut + out_cols]
        rain_now = rain_ext[inner_cut : inner_cut + out_rows, inner_cut : inner_cut + out_cols]
        fresh, water_new = advance(current, erod_now, row_ok_now, col_ok_now)
        keep = margin - 2
        own_water = water_new[keep : keep + rows_own, keep : keep + cols_own]
        mean_water = butterfly_sum(jnp.sum(own_water * own_water)) / cells
        current = settle(fresh, rain_now, mean_water)
    return current


def solution(mesh):
    in_specs = (P(None, "rows", "cols"), P("rows", "cols"), P("rows", "cols"))
    out_specs = P(None, "rows", "cols")
    return jax.shard_map(shards, mesh=mesh, in_specs=in_specs, out_specs=out_specs, check_vma=False)
```

```python
import jax
import jax.numpy as jnp
from jax import lax
from jax.sharding import PartitionSpec as P

STEPS = 8


time_step = 0.25
wet_floor = 0.05
deep_floor = 0.1
carry_coef = 0.4
cap_floor = 0.0025
erode_coef = 0.3
settle_coef = 0.3
slide_coef = 0.1
talus_drop = 0.5
talus_sharp = 4.0
evap_coef = 0.05
rain_depth = 0.1
rock_rates = (1.0, 0.6, 0.3, 0.12)


def with_halo(x, sides, width):
    for axis, dim in sides:
        count, length = (lax.axis_size(axis), x.shape[dim])
        up = [(i, (i + 1) % count) for i in range(count - 1)]
        down = [(j, i) for i, j in up]
        last = lax.slice_in_dim(x, length - width, length, axis=dim)
        first = lax.slice_in_dim(x, 0, width, axis=dim)
        before = lax.ppermute(last, axis, up)
        after = lax.ppermute(first, axis, down)
        x = jnp.concatenate([before, x, after], axis=dim)
    return x


def rock_rate(classes):
    result = rock_rates[0] * (classes == 0).astype(jnp.float32)
    for klass in range(1, 4):
        result = result + rock_rates[klass] * (classes == klass).astype(jnp.float32)
    return result


def talus_flow(diff):
    return (
        jax.nn.softplus(talus_sharp * (diff - talus_drop))
        - jax.nn.softplus(talus_sharp * (-diff - talus_drop))
    ) / talus_sharp


def advance(padded, erod, row_ok, col_ok):
    rows_out = padded.shape[1] - 4
    cols_out = padded.shape[2] - 4

    def inner(field, row_step, col_step):
        return field[
            ..., 1 + row_step : 3 + row_step + rows_out, 1 + col_step : 3 + col_step + cols_out
        ]

    def middle(field, row_step, col_step):
        return field[1 + row_step : 1 + row_step + rows_out, 1 + col_step : 1 + col_step + cols_out]

    def core(field, row_step, col_step):
        return field[
            ..., 2 + row_step : 2 + row_step + rows_out, 2 + col_step : 2 + col_step + cols_out
        ]

    height = padded[0]
    water_now = padded[1]
    surface = height + water_now
    inside = row_ok[1 : 3 + rows_out][:, None] * col_ok[1 : 3 + cols_out][None, :]
    left_ok = col_ok[0 : 2 + cols_out][None, :]
    right_ok = col_ok[2 : 4 + cols_out][None, :]
    upper_ok = row_ok[0 : 2 + rows_out][:, None]
    lower_ok = row_ok[2 : 4 + rows_out][:, None]
    centre = inner(surface, 0, 0)
    to_left = (
        jnp.maximum(0.0, inner(padded[3], 0, 0) + time_step * (centre - inner(surface, 0, -1)))
        * left_ok
        * inside
    )
    to_right = (
        jnp.maximum(0.0, inner(padded[4], 0, 0) + time_step * (centre - inner(surface, 0, 1)))
        * right_ok
        * inside
    )
    to_upper = (
        jnp.maximum(0.0, inner(padded[5], 0, 0) + time_step * (centre - inner(surface, -1, 0)))
        * upper_ok
        * inside
    )
    to_lower = (
        jnp.maximum(0.0, inner(padded[6], 0, 0) + time_step * (centre - inner(surface, 1, 0)))
        * lower_ok
        * inside
    )
    raw_total = to_left + to_right + to_upper + to_lower
    limiter = jnp.minimum(
        1.0, inner(water_now, 0, 0) / jnp.maximum(time_step * raw_total, wet_floor)
    )
    to_left = to_left * limiter
    to_right = to_right * limiter
    to_upper = to_upper * limiter
    to_lower = to_lower * limiter
    carried = inner(padded[2], 0, 0) / jnp.maximum(inner(water_now, 0, 0), deep_floor)
    outflow = (
        middle(to_left, 0, 0)
        + middle(to_right, 0, 0)
        + middle(to_upper, 0, 0)
        + middle(to_lower, 0, 0)
    )
    inflow = (
        middle(to_right, 0, -1)
        + middle(to_left, 0, 1)
        + middle(to_lower, -1, 0)
        + middle(to_upper, 1, 0)
    )
    water_old = core(water_now, 0, 0)
    water_new = water_old + time_step * (inflow - outflow)
    to_left, to_right, to_upper, to_lower, water_new = lax.optimization_barrier(
        (to_left, to_right, to_upper, to_lower, water_new)
    )
    across = 0.5 * (
        middle(to_right, 0, -1)
        - middle(to_left, 0, 0)
        + middle(to_right, 0, 0)
        - middle(to_left, 0, 1)
    )
    along = 0.5 * (
        middle(to_lower, -1, 0)
        - middle(to_upper, 0, 0)
        + middle(to_lower, 0, 0)
        - middle(to_upper, 1, 0)
    )
    mean_depth = jnp.maximum(0.5 * (water_old + water_new), deep_floor)
    speed_u = padded[7]
    speed_v = padded[8]
    smooth_u = (
        4.0 * core(speed_u, 0, 0)
        + core(speed_u, 0, -1)
        + core(speed_u, 0, 1)
        + core(speed_u, -1, 0)
        + core(speed_u, 1, 0)
    ) / 16.0
    smooth_v = (
        4.0 * core(speed_v, 0, 0)
        + core(speed_v, 0, -1)
        + core(speed_v, 0, 1)
        + core(speed_v, -1, 0)
        + core(speed_v, 1, 0)
    ) / 16.0
    new_u = across / (2.0 * mean_depth) + smooth_u
    new_v = along / (2.0 * mean_depth) + smooth_v
    sediment = core(padded[2], 0, 0) + time_step * (
        middle(to_right, 0, -1) * middle(carried, 0, -1)
        + middle(to_left, 0, 1) * middle(carried, 0, 1)
        + middle(to_lower, -1, 0) * middle(carried, -1, 0)
        + middle(to_upper, 1, 0) * middle(carried, 1, 0)
        - outflow * middle(carried, 0, 0)
    )
    left_in = col_ok[1 : 1 + cols_out][None, :]
    right_in = col_ok[3 : 3 + cols_out][None, :]
    upper_in = row_ok[1 : 1 + rows_out][:, None]
    lower_in = row_ok[3 : 3 + rows_out][:, None]
    base = core(height, 0, 0)
    diff_left = core(height, 0, -1) - base
    diff_right = core(height, 0, 1) - base
    diff_upper = core(height, -1, 0) - base
    diff_lower = core(height, 1, 0) - base
    grad_x = 0.5 * (right_in * diff_right - left_in * diff_left)
    grad_y = 0.5 * (lower_in * diff_lower - upper_in * diff_upper)
    grad_sq = grad_x * grad_x + grad_y * grad_y
    capacity = carry_coef * jnp.sqrt(
        (new_u * new_u + new_v * new_v) * grad_sq / (1.0 + grad_sq) + cap_floor
    )
    gap_left = capacity - sediment
    delta = jnp.where(gap_left > 0.0, erode_coef * erod * gap_left, settle_coef * gap_left)
    thermal = slide_coef * (
        left_in * talus_flow(diff_left)
        + right_in * talus_flow(diff_right)
        + upper_in * talus_flow(diff_upper)
        + lower_in * talus_flow(diff_lower)
    )
    new_height = base - delta + thermal
    new_sediment = sediment + delta
    out_ok = row_ok[2 : 2 + rows_out][:, None] * col_ok[2 : 2 + cols_out][None, :]
    fresh = jnp.stack(
        [
            new_height,
            water_new,
            new_sediment,
            middle(to_left, 0, 0),
            middle(to_right, 0, 0),
            middle(to_upper, 0, 0),
            middle(to_lower, 0, 0),
            new_u,
            new_v,
        ]
    )
    return fresh * out_ok[None], water_new


def settle(fresh, rain_field, mean_water):
    return fresh.at[1].set(fresh[1] * (1.0 - evap_coef * mean_water) + rain_depth * rain_field)


def valid_line(index, extent, whole, margin):
    places = index * extent + jnp.arange(-margin, extent + margin, dtype=jnp.int32)
    return ((places >= 0) & (places < whole)).astype(jnp.float32)


def flip_pairs(count, partner):
    return [(i, partner(i)) for i in range(count)]


def quad_pairs(count, stride, shift):
    return [
        (i, i - ((i // stride) % 4) * stride + (((i // stride) % 4 + shift) % 4) * stride)
        for i in range(count)
    ]


def butterfly_sum(value):
    rows = lax.axis_size("rows")
    cols = lax.axis_size("cols")
    total = jnp.broadcast_to(value, (1, 128))
    total = total + lax.ppermute(total, "cols", flip_pairs(cols, lambda c: c ^ 1))
    for axis, count, stride, extra in (
        ("rows", rows, 1, None),
        ("rows", rows, 4, "pair"),
        ("rows", rows, 8, None),
        ("cols", cols, 2, None),
    ):
        if extra == "pair":
            total = total + lax.ppermute(total, axis, flip_pairs(count, lambda r: r ^ stride))
            continue
        part = total
        for shift in (1, 2, 3):
            part = part + lax.ppermute(total, axis, quad_pairs(count, stride, shift))
        total = part
    return total[0, 0]


def shards(state, hardness, rain_mask):
    rows_own = state.shape[1]
    cols_own = state.shape[2]
    whole_rows = rows_own * lax.axis_size("rows")
    whole_cols = cols_own * lax.axis_size("cols")
    cells = float(whole_rows * whole_cols)
    row_index = lax.axis_index("rows")
    col_index = lax.axis_index("cols")
    erod_own = rock_rate(hardness)
    rain_own = rain_mask.astype(jnp.float32)
    width = 2 * STEPS
    stacked = jnp.concatenate([state, erod_own[None], rain_own[None]], axis=0)
    stacked = with_halo(stacked, (("rows", 1), ("cols", 2)), width)
    current = stacked[:9]
    erod_ext = stacked[9]
    rain_ext = stacked[10]
    row_ok = valid_line(row_index, rows_own, whole_rows, width)
    col_ok = valid_line(col_index, cols_own, whole_cols, width)
    for step in range(STEPS):
        margin = width - 2 * step
        cut = 2 * step
        row_ok_now = row_ok[cut : cut + rows_own + 2 * margin]
        col_ok_now = col_ok[cut : cut + cols_own + 2 * margin]
        inner_cut = cut + 2
        out_rows = rows_own + 2 * margin - 4
        out_cols = cols_own + 2 * margin - 4
        erod_now = erod_ext[inner_cut : inner_cut + out_rows, inner_cut : inner_cut + out_cols]
        rain_now = rain_ext[inner_cut : inner_cut + out_rows, inner_cut : inner_cut + out_cols]
        fresh, water_new = advance(current, erod_now, row_ok_now, col_ok_now)
        keep = margin - 2
        own_water = water_new[keep : keep + rows_own, keep : keep + cols_own]
        mean_water = butterfly_sum(jnp.sum(own_water * own_water)) / cells
        current = settle(fresh, rain_now, mean_water)
    return current


def solution(mesh):
    in_specs = (P(None, "rows", "cols"), P("rows", "cols"), P("rows", "cols"))
    out_specs = P(None, "rows", "cols")
    return jax.shard_map(shards, mesh=mesh, in_specs=in_specs, out_specs=out_specs, check_vma=False)
```

```python
import jax
import jax.numpy as jnp
from jax import lax
from jax.sharding import PartitionSpec as P

STEPS = 8


time_step = 0.25
wet_floor = 0.05
deep_floor = 0.1
carry_coef = 0.4
cap_floor = 0.0025
erode_coef = 0.3
settle_coef = 0.3
slide_coef = 0.1
talus_drop = 0.5
talus_sharp = 4.0
evap_coef = 0.05
rain_depth = 0.1
rock_rates = (1.0, 0.6, 0.3, 0.12)


def with_halo(x, sides, width):
    for axis, dim in sides:
        count, length = (lax.axis_size(axis), x.shape[dim])
        up = [(i, (i + 1) % count) for i in range(count - 1)]
        down = [(j, i) for i, j in up]
        last = lax.slice_in_dim(x, length - width, length, axis=dim)
        first = lax.slice_in_dim(x, 0, width, axis=dim)
        before = lax.ppermute(last, axis, up)
        after = lax.ppermute(first, axis, down)
        x = jnp.concatenate([before, x, after], axis=dim)
    return x


def rock_rate(classes):
    result = rock_rates[0] * (classes == 0).astype(jnp.float32)
    for klass in range(1, 4):
        result = result + rock_rates[klass] * (classes == klass).astype(jnp.float32)
    return result


def talus_flow(diff):
    return (
        jax.nn.softplus(talus_sharp * (diff - talus_drop))
        - jax.nn.softplus(talus_sharp * (-diff - talus_drop))
    ) / talus_sharp


def advance(padded, erod, row_ok, col_ok):
    rows_out = padded.shape[1] - 4
    cols_out = padded.shape[2] - 4

    def inner(field, row_step, col_step):
        return field[
            ..., 1 + row_step : 3 + row_step + rows_out, 1 + col_step : 3 + col_step + cols_out
        ]

    def middle(field, row_step, col_step):
        return field[1 + row_step : 1 + row_step + rows_out, 1 + col_step : 1 + col_step + cols_out]

    def core(field, row_step, col_step):
        return field[
            ..., 2 + row_step : 2 + row_step + rows_out, 2 + col_step : 2 + col_step + cols_out
        ]

    height = padded[0]
    water_now = padded[1]
    surface = height + water_now
    inside = row_ok[1 : 3 + rows_out][:, None] * col_ok[1 : 3 + cols_out][None, :]
    left_ok = col_ok[0 : 2 + cols_out][None, :]
    right_ok = col_ok[2 : 4 + cols_out][None, :]
    upper_ok = row_ok[0 : 2 + rows_out][:, None]
    lower_ok = row_ok[2 : 4 + rows_out][:, None]
    centre = inner(surface, 0, 0)
    to_left = (
        jnp.maximum(0.0, inner(padded[3], 0, 0) + time_step * (centre - inner(surface, 0, -1)))
        * left_ok
        * inside
    )
    to_right = (
        jnp.maximum(0.0, inner(padded[4], 0, 0) + time_step * (centre - inner(surface, 0, 1)))
        * right_ok
        * inside
    )
    to_upper = (
        jnp.maximum(0.0, inner(padded[5], 0, 0) + time_step * (centre - inner(surface, -1, 0)))
        * upper_ok
        * inside
    )
    to_lower = (
        jnp.maximum(0.0, inner(padded[6], 0, 0) + time_step * (centre - inner(surface, 1, 0)))
        * lower_ok
        * inside
    )
    raw_total = to_left + to_right + to_upper + to_lower
    limiter = jnp.minimum(
        1.0, inner(water_now, 0, 0) / jnp.maximum(time_step * raw_total, wet_floor)
    )
    to_left = to_left * limiter
    to_right = to_right * limiter
    to_upper = to_upper * limiter
    to_lower = to_lower * limiter
    carried = inner(padded[2], 0, 0) / jnp.maximum(inner(water_now, 0, 0), deep_floor)
    outflow = (
        middle(to_left, 0, 0)
        + middle(to_right, 0, 0)
        + middle(to_upper, 0, 0)
        + middle(to_lower, 0, 0)
    )
    inflow = (
        middle(to_right, 0, -1)
        + middle(to_left, 0, 1)
        + middle(to_lower, -1, 0)
        + middle(to_upper, 1, 0)
    )
    water_old = core(water_now, 0, 0)
    water_new = water_old + time_step * (inflow - outflow)
    to_left, to_right, to_upper, to_lower, water_new = lax.optimization_barrier(
        (to_left, to_right, to_upper, to_lower, water_new)
    )
    across = 0.5 * (
        middle(to_right, 0, -1)
        - middle(to_left, 0, 0)
        + middle(to_right, 0, 0)
        - middle(to_left, 0, 1)
    )
    along = 0.5 * (
        middle(to_lower, -1, 0)
        - middle(to_upper, 0, 0)
        + middle(to_lower, 0, 0)
        - middle(to_upper, 1, 0)
    )
    mean_depth = jnp.maximum(0.5 * (water_old + water_new), deep_floor)
    speed_u = padded[7]
    speed_v = padded[8]
    smooth_u = (
        4.0 * core(speed_u, 0, 0)
        + core(speed_u, 0, -1)
        + core(speed_u, 0, 1)
        + core(speed_u, -1, 0)
        + core(speed_u, 1, 0)
    ) / 16.0
    smooth_v = (
        4.0 * core(speed_v, 0, 0)
        + core(speed_v, 0, -1)
        + core(speed_v, 0, 1)
        + core(speed_v, -1, 0)
        + core(speed_v, 1, 0)
    ) / 16.0
    new_u = across / (2.0 * mean_depth) + smooth_u
    new_v = along / (2.0 * mean_depth) + smooth_v
    sediment = core(padded[2], 0, 0) + time_step * (
        middle(to_right, 0, -1) * middle(carried, 0, -1)
        + middle(to_left, 0, 1) * middle(carried, 0, 1)
        + middle(to_lower, -1, 0) * middle(carried, -1, 0)
        + middle(to_upper, 1, 0) * middle(carried, 1, 0)
        - outflow * middle(carried, 0, 0)
    )
    left_in = col_ok[1 : 1 + cols_out][None, :]
    right_in = col_ok[3 : 3 + cols_out][None, :]
    upper_in = row_ok[1 : 1 + rows_out][:, None]
    lower_in = row_ok[3 : 3 + rows_out][:, None]
    base = core(height, 0, 0)
    diff_left = core(height, 0, -1) - base
    diff_right = core(height, 0, 1) - base
    diff_upper = core(height, -1, 0) - base
    diff_lower = core(height, 1, 0) - base
    grad_x = 0.5 * (right_in * diff_right - left_in * diff_left)
    grad_y = 0.5 * (lower_in * diff_lower - upper_in * diff_upper)
    grad_sq = grad_x * grad_x + grad_y * grad_y
    capacity = carry_coef * jnp.sqrt(
        (new_u * new_u + new_v * new_v) * grad_sq / (1.0 + grad_sq) + cap_floor
    )
    gap_left = capacity - sediment
    delta = jnp.where(gap_left > 0.0, erode_coef * erod * gap_left, settle_coef * gap_left)
    thermal = slide_coef * (
        left_in * talus_flow(diff_left)
        + right_in * talus_flow(diff_right)
        + upper_in * talus_flow(diff_upper)
        + lower_in * talus_flow(diff_lower)
    )
    new_height = base - delta + thermal
    new_sediment = sediment + delta
    out_ok = row_ok[2 : 2 + rows_out][:, None] * col_ok[2 : 2 + cols_out][None, :]
    fresh = jnp.stack(
        [
            new_height,
            water_new,
            new_sediment,
            middle(to_left, 0, 0),
            middle(to_right, 0, 0),
            middle(to_upper, 0, 0),
            middle(to_lower, 0, 0),
            new_u,
            new_v,
        ]
    )
    return fresh * out_ok[None], water_new


def settle(fresh, rain_field, mean_water):
    return fresh.at[1].set(fresh[1] * (1.0 - evap_coef * mean_water) + rain_depth * rain_field)


def valid_line(index, extent, whole, margin):
    places = index * extent + jnp.arange(-margin, extent + margin, dtype=jnp.int32)
    return ((places >= 0) & (places < whole)).astype(jnp.float32)


def flip_pairs(count, partner):
    return [(i, partner(i)) for i in range(count)]


def quad_pairs(count, stride, shift):
    return [
        (i, i - ((i // stride) % 4) * stride + (((i // stride) % 4 + shift) % 4) * stride)
        for i in range(count)
    ]


def butterfly_sum(value):
    rows = lax.axis_size("rows")
    cols = lax.axis_size("cols")
    total = jnp.broadcast_to(value, (1, 128))
    part = total
    for flip_r, flip_c in ((0, 1), (4, 0), (4, 1)):
        pairs = [(r * cols + c, (r ^ flip_r) * cols + (c ^ flip_c)) for r in range(rows) for c in range(cols)]
        part = part + lax.ppermute(total, ("rows", "cols"), pairs)
    total = part
    for axis, count, stride in (("rows", rows, 1), ("rows", rows, 8), ("cols", cols, 2)):
        part = total
        for shift in (1, 2, 3):
            part = part + lax.ppermute(total, axis, quad_pairs(count, stride, shift))
        total = part
    return total[0, 0]


def shards(state, hardness, rain_mask):
    rows_own = state.shape[1]
    cols_own = state.shape[2]
    whole_rows = rows_own * lax.axis_size("rows")
    whole_cols = cols_own * lax.axis_size("cols")
    cells = float(whole_rows * whole_cols)
    row_index = lax.axis_index("rows")
    col_index = lax.axis_index("cols")
    erod_own = rock_rate(hardness)
    rain_own = rain_mask.astype(jnp.float32)
    width = 2 * STEPS
    stacked = jnp.concatenate([state, erod_own[None], rain_own[None]], axis=0)
    stacked = with_halo(stacked, (("rows", 1), ("cols", 2)), width)
    current = stacked[:9]
    erod_ext = stacked[9]
    rain_ext = stacked[10]
    row_ok = valid_line(row_index, rows_own, whole_rows, width)
    col_ok = valid_line(col_index, cols_own, whole_cols, width)
    for step in range(STEPS):
        margin = width - 2 * step
        cut = 2 * step
        row_ok_now = row_ok[cut : cut + rows_own + 2 * margin]
        col_ok_now = col_ok[cut : cut + cols_own + 2 * margin]
        inner_cut = cut + 2
        out_rows = rows_own + 2 * margin - 4
        out_cols = cols_own + 2 * margin - 4
        erod_now = erod_ext[inner_cut : inner_cut + out_rows, inner_cut : inner_cut + out_cols]
        rain_now = rain_ext[inner_cut : inner_cut + out_rows, inner_cut : inner_cut + out_cols]
        fresh, water_new = advance(current, erod_now, row_ok_now, col_ok_now)
        keep = margin - 2
        own_water = water_new[keep : keep + rows_own, keep : keep + cols_own]
        mean_water = butterfly_sum(jnp.sum(own_water * own_water)) / cells
        current = settle(fresh, rain_now, mean_water)
    return current


def solution(mesh):
    in_specs = (P(None, "rows", "cols"), P("rows", "cols"), P("rows", "cols"))
    out_specs = P(None, "rows", "cols")
    return jax.shard_map(shards, mesh=mesh, in_specs=in_specs, out_specs=out_specs, check_vma=False)
```

```python
import jax
import jax.numpy as jnp
from jax import lax
from jax.sharding import PartitionSpec as P

STEPS = 8


time_step = 0.25
wet_floor = 0.05
deep_floor = 0.1
carry_coef = 0.4
cap_floor = 0.0025
erode_coef = 0.3
settle_coef = 0.3
slide_coef = 0.1
talus_drop = 0.5
talus_sharp = 4.0
evap_coef = 0.05
rain_depth = 0.1
rock_rates = (1.0, 0.6, 0.3, 0.12)


def with_halo(x, sides, width):
    for axis, dim in sides:
        count, length = (lax.axis_size(axis), x.shape[dim])
        up = [(i, (i + 1) % count) for i in range(count - 1)]
        down = [(j, i) for i, j in up]
        last = lax.slice_in_dim(x, length - width, length, axis=dim)
        first = lax.slice_in_dim(x, 0, width, axis=dim)
        before = lax.ppermute(last, axis, up)
        after = lax.ppermute(first, axis, down)
        x = jnp.concatenate([before, x, after], axis=dim)
    return x


def rock_rate(classes):
    result = rock_rates[0] * (classes == 0).astype(jnp.float32)
    for klass in range(1, 4):
        result = result + rock_rates[klass] * (classes == klass).astype(jnp.float32)
    return result


def talus_flow(diff):
    return (
        jax.nn.softplus(talus_sharp * (diff - talus_drop))
        - jax.nn.softplus(talus_sharp * (-diff - talus_drop))
    ) / talus_sharp


def advance(padded, erod, row_ok, col_ok):
    rows_out = padded.shape[1] - 4
    cols_out = padded.shape[2] - 4

    def inner(field, row_step, col_step):
        return field[
            ..., 1 + row_step : 3 + row_step + rows_out, 1 + col_step : 3 + col_step + cols_out
        ]

    def middle(field, row_step, col_step):
        return field[1 + row_step : 1 + row_step + rows_out, 1 + col_step : 1 + col_step + cols_out]

    def core(field, row_step, col_step):
        return field[
            ..., 2 + row_step : 2 + row_step + rows_out, 2 + col_step : 2 + col_step + cols_out
        ]

    height = padded[0]
    water_now = padded[1]
    surface = height + water_now
    inside = row_ok[1 : 3 + rows_out][:, None] * col_ok[1 : 3 + cols_out][None, :]
    left_ok = col_ok[0 : 2 + cols_out][None, :]
    right_ok = col_ok[2 : 4 + cols_out][None, :]
    upper_ok = row_ok[0 : 2 + rows_out][:, None]
    lower_ok = row_ok[2 : 4 + rows_out][:, None]
    centre = inner(surface, 0, 0)
    to_left = (
        jnp.maximum(0.0, inner(padded[3], 0, 0) + time_step * (centre - inner(surface, 0, -1)))
        * left_ok
        * inside
    )
    to_right = (
        jnp.maximum(0.0, inner(padded[4], 0, 0) + time_step * (centre - inner(surface, 0, 1)))
        * right_ok
        * inside
    )
    to_upper = (
        jnp.maximum(0.0, inner(padded[5], 0, 0) + time_step * (centre - inner(surface, -1, 0)))
        * upper_ok
        * inside
    )
    to_lower = (
        jnp.maximum(0.0, inner(padded[6], 0, 0) + time_step * (centre - inner(surface, 1, 0)))
        * lower_ok
        * inside
    )
    raw_total = to_left + to_right + to_upper + to_lower
    limiter = jnp.minimum(
        1.0, inner(water_now, 0, 0) / jnp.maximum(time_step * raw_total, wet_floor)
    )
    to_left = to_left * limiter
    to_right = to_right * limiter
    to_upper = to_upper * limiter
    to_lower = to_lower * limiter
    carried = inner(padded[2], 0, 0) / jnp.maximum(inner(water_now, 0, 0), deep_floor)
    outflow = (
        middle(to_left, 0, 0)
        + middle(to_right, 0, 0)
        + middle(to_upper, 0, 0)
        + middle(to_lower, 0, 0)
    )
    inflow = (
        middle(to_right, 0, -1)
        + middle(to_left, 0, 1)
        + middle(to_lower, -1, 0)
        + middle(to_upper, 1, 0)
    )
    water_old = core(water_now, 0, 0)
    water_new = water_old + time_step * (inflow - outflow)
    to_left, to_right, to_upper, to_lower, water_new = lax.optimization_barrier(
        (to_left, to_right, to_upper, to_lower, water_new)
    )
    across = 0.5 * (
        middle(to_right, 0, -1)
        - middle(to_left, 0, 0)
        + middle(to_right, 0, 0)
        - middle(to_left, 0, 1)
    )
    along = 0.5 * (
        middle(to_lower, -1, 0)
        - middle(to_upper, 0, 0)
        + middle(to_lower, 0, 0)
        - middle(to_upper, 1, 0)
    )
    mean_depth = jnp.maximum(0.5 * (water_old + water_new), deep_floor)
    speed_u = padded[7]
    speed_v = padded[8]
    smooth_u = (
        4.0 * core(speed_u, 0, 0)
        + core(speed_u, 0, -1)
        + core(speed_u, 0, 1)
        + core(speed_u, -1, 0)
        + core(speed_u, 1, 0)
    ) / 16.0
    smooth_v = (
        4.0 * core(speed_v, 0, 0)
        + core(speed_v, 0, -1)
        + core(speed_v, 0, 1)
        + core(speed_v, -1, 0)
        + core(speed_v, 1, 0)
    ) / 16.0
    new_u = across / (2.0 * mean_depth) + smooth_u
    new_v = along / (2.0 * mean_depth) + smooth_v
    sediment = core(padded[2], 0, 0) + time_step * (
        middle(to_right, 0, -1) * middle(carried, 0, -1)
        + middle(to_left, 0, 1) * middle(carried, 0, 1)
        + middle(to_lower, -1, 0) * middle(carried, -1, 0)
        + middle(to_upper, 1, 0) * middle(carried, 1, 0)
        - outflow * middle(carried, 0, 0)
    )
    left_in = col_ok[1 : 1 + cols_out][None, :]
    right_in = col_ok[3 : 3 + cols_out][None, :]
    upper_in = row_ok[1 : 1 + rows_out][:, None]
    lower_in = row_ok[3 : 3 + rows_out][:, None]
    base = core(height, 0, 0)
    diff_left = core(height, 0, -1) - base
    diff_right = core(height, 0, 1) - base
    diff_upper = core(height, -1, 0) - base
    diff_lower = core(height, 1, 0) - base
    grad_x = 0.5 * (right_in * diff_right - left_in * diff_left)
    grad_y = 0.5 * (lower_in * diff_lower - upper_in * diff_upper)
    grad_sq = grad_x * grad_x + grad_y * grad_y
    capacity = carry_coef * jnp.sqrt(
        (new_u * new_u + new_v * new_v) * grad_sq / (1.0 + grad_sq) + cap_floor
    )
    gap_left = capacity - sediment
    delta = jnp.where(gap_left > 0.0, erode_coef * erod * gap_left, settle_coef * gap_left)
    thermal = slide_coef * (
        left_in * talus_flow(diff_left)
        + right_in * talus_flow(diff_right)
        + upper_in * talus_flow(diff_upper)
        + lower_in * talus_flow(diff_lower)
    )
    new_height = base - delta + thermal
    new_sediment = sediment + delta
    out_ok = row_ok[2 : 2 + rows_out][:, None] * col_ok[2 : 2 + cols_out][None, :]
    fresh = jnp.stack(
        [
            new_height,
            water_new,
            new_sediment,
            middle(to_left, 0, 0),
            middle(to_right, 0, 0),
            middle(to_upper, 0, 0),
            middle(to_lower, 0, 0),
            new_u,
            new_v,
        ]
    )
    return fresh * out_ok[None], water_new


def settle(fresh, rain_field, mean_water):
    return fresh.at[1].set(fresh[1] * (1.0 - evap_coef * mean_water) + rain_depth * rain_field)


def valid_line(index, extent, whole, margin):
    places = index * extent + jnp.arange(-margin, extent + margin, dtype=jnp.int32)
    return ((places >= 0) & (places < whole)).astype(jnp.float32)


def flip_pairs(count, partner):
    return [(i, partner(i)) for i in range(count)]


def quad_pairs(count, stride, shift):
    return [
        (i, i - ((i // stride) % 4) * stride + (((i // stride) % 4 + shift) % 4) * stride)
        for i in range(count)
    ]


def butterfly_sum(value):
    rows = lax.axis_size("rows")
    cols = lax.axis_size("cols")
    total = jnp.broadcast_to(value, (1, 128))
    part = total
    for flip_r, flip_c in ((0, 1), (4, 0), (4, 1)):
        pairs = [(r * cols + c, (r ^ flip_r) * cols + (c ^ flip_c)) for r in range(rows) for c in range(cols)]
        part = part + lax.ppermute(total, ("rows", "cols"), pairs)
    total = part
    for axis, count, stride in (("rows", rows, 1), ("rows", rows, 8), ("cols", cols, 2)):
        part = total
        for shift in (1, 3, 2):
            part = part + lax.ppermute(total, axis, quad_pairs(count, stride, shift))
        total = part
    return total[0, 0]


def shards(state, hardness, rain_mask):
    rows_own = state.shape[1]
    cols_own = state.shape[2]
    whole_rows = rows_own * lax.axis_size("rows")
    whole_cols = cols_own * lax.axis_size("cols")
    cells = float(whole_rows * whole_cols)
    row_index = lax.axis_index("rows")
    col_index = lax.axis_index("cols")
    erod_own = rock_rate(hardness)
    rain_own = rain_mask.astype(jnp.float32)
    width = 2 * STEPS
    stacked = jnp.concatenate([state, erod_own[None], rain_own[None]], axis=0)
    stacked = with_halo(stacked, (("rows", 1), ("cols", 2)), width)
    current = stacked[:9]
    erod_ext = stacked[9]
    rain_ext = stacked[10]
    row_ok = valid_line(row_index, rows_own, whole_rows, width)
    col_ok = valid_line(col_index, cols_own, whole_cols, width)
    for step in range(STEPS):
        margin = width - 2 * step
        cut = 2 * step
        row_ok_now = row_ok[cut : cut + rows_own + 2 * margin]
        col_ok_now = col_ok[cut : cut + cols_own + 2 * margin]
        inner_cut = cut + 2
        out_rows = rows_own + 2 * margin - 4
        out_cols = cols_own + 2 * margin - 4
        erod_now = erod_ext[inner_cut : inner_cut + out_rows, inner_cut : inner_cut + out_cols]
        rain_now = rain_ext[inner_cut : inner_cut + out_rows, inner_cut : inner_cut + out_cols]
        fresh, water_new = advance(current, erod_now, row_ok_now, col_ok_now)
        keep = margin - 2
        own_water = water_new[keep : keep + rows_own, keep : keep + cols_own]
        mean_water = butterfly_sum(jnp.sum(own_water * own_water)) / cells
        current = settle(fresh, rain_now, mean_water)
    return current


def solution(mesh):
    in_specs = (P(None, "rows", "cols"), P("rows", "cols"), P("rows", "cols"))
    out_specs = P(None, "rows", "cols")
    return jax.shard_map(shards, mesh=mesh, in_specs=in_specs, out_specs=out_specs, check_vma=False)
```

```python
import jax
import jax.numpy as jnp
from jax import lax
from jax.sharding import PartitionSpec as P

STEPS = 8


time_step = 0.25
wet_floor = 0.05
deep_floor = 0.1
carry_coef = 0.4
cap_floor = 0.0025
erode_coef = 0.3
settle_coef = 0.3
slide_coef = 0.1
talus_drop = 0.5
talus_sharp = 4.0
evap_coef = 0.05
rain_depth = 0.1
rock_rates = (1.0, 0.6, 0.3, 0.12)


def with_halo(x, sides, width):
    for axis, dim in sides:
        count, length = (lax.axis_size(axis), x.shape[dim])
        up = [(i, (i + 1) % count) for i in range(count - 1)]
        down = [(j, i) for i, j in up]
        last = lax.slice_in_dim(x, length - width, length, axis=dim)
        first = lax.slice_in_dim(x, 0, width, axis=dim)
        before = lax.ppermute(last, axis, up)
        after = lax.ppermute(first, axis, down)
        x = jnp.concatenate([before, x, after], axis=dim)
    return x


def rock_rate(classes):
    result = rock_rates[0] * (classes == 0).astype(jnp.float32)
    for klass in range(1, 4):
        result = result + rock_rates[klass] * (classes == klass).astype(jnp.float32)
    return result


def talus_flow(diff):
    return (
        jax.nn.softplus(talus_sharp * (diff - talus_drop))
        - jax.nn.softplus(talus_sharp * (-diff - talus_drop))
    ) / talus_sharp


def advance(padded, erod, row_ok, col_ok):
    rows_out = padded.shape[1] - 4
    cols_out = padded.shape[2] - 4

    def inner(field, row_step, col_step):
        return field[
            ..., 1 + row_step : 3 + row_step + rows_out, 1 + col_step : 3 + col_step + cols_out
        ]

    def middle(field, row_step, col_step):
        return field[1 + row_step : 1 + row_step + rows_out, 1 + col_step : 1 + col_step + cols_out]

    def core(field, row_step, col_step):
        return field[
            ..., 2 + row_step : 2 + row_step + rows_out, 2 + col_step : 2 + col_step + cols_out
        ]

    height = padded[0]
    water_now = padded[1]
    surface = height + water_now
    inside = row_ok[1 : 3 + rows_out][:, None] * col_ok[1 : 3 + cols_out][None, :]
    left_ok = col_ok[0 : 2 + cols_out][None, :]
    right_ok = col_ok[2 : 4 + cols_out][None, :]
    upper_ok = row_ok[0 : 2 + rows_out][:, None]
    lower_ok = row_ok[2 : 4 + rows_out][:, None]
    centre = inner(surface, 0, 0)
    to_left = (
        jnp.maximum(0.0, inner(padded[3], 0, 0) + time_step * (centre - inner(surface, 0, -1)))
        * left_ok
        * inside
    )
    to_right = (
        jnp.maximum(0.0, inner(padded[4], 0, 0) + time_step * (centre - inner(surface, 0, 1)))
        * right_ok
        * inside
    )
    to_upper = (
        jnp.maximum(0.0, inner(padded[5], 0, 0) + time_step * (centre - inner(surface, -1, 0)))
        * upper_ok
        * inside
    )
    to_lower = (
        jnp.maximum(0.0, inner(padded[6], 0, 0) + time_step * (centre - inner(surface, 1, 0)))
        * lower_ok
        * inside
    )
    raw_total = to_left + to_right + to_upper + to_lower
    limiter = jnp.minimum(
        1.0, inner(water_now, 0, 0) / jnp.maximum(time_step * raw_total, wet_floor)
    )
    to_left = to_left * limiter
    to_right = to_right * limiter
    to_upper = to_upper * limiter
    to_lower = to_lower * limiter
    carried = inner(padded[2], 0, 0) / jnp.maximum(inner(water_now, 0, 0), deep_floor)
    outflow = (
        middle(to_left, 0, 0)
        + middle(to_right, 0, 0)
        + middle(to_upper, 0, 0)
        + middle(to_lower, 0, 0)
    )
    inflow = (
        middle(to_right, 0, -1)
        + middle(to_left, 0, 1)
        + middle(to_lower, -1, 0)
        + middle(to_upper, 1, 0)
    )
    water_old = core(water_now, 0, 0)
    water_new = water_old + time_step * (inflow - outflow)
    to_left, to_right, to_upper, to_lower, water_new = lax.optimization_barrier(
        (to_left, to_right, to_upper, to_lower, water_new)
    )
    across = 0.5 * (
        middle(to_right, 0, -1)
        - middle(to_left, 0, 0)
        + middle(to_right, 0, 0)
        - middle(to_left, 0, 1)
    )
    along = 0.5 * (
        middle(to_lower, -1, 0)
        - middle(to_upper, 0, 0)
        + middle(to_lower, 0, 0)
        - middle(to_upper, 1, 0)
    )
    mean_depth = jnp.maximum(0.5 * (water_old + water_new), deep_floor)
    speed_u = padded[7]
    speed_v = padded[8]
    smooth_u = (
        4.0 * core(speed_u, 0, 0)
        + core(speed_u, 0, -1)
        + core(speed_u, 0, 1)
        + core(speed_u, -1, 0)
        + core(speed_u, 1, 0)
    ) / 16.0
    smooth_v = (
        4.0 * core(speed_v, 0, 0)
        + core(speed_v, 0, -1)
        + core(speed_v, 0, 1)
        + core(speed_v, -1, 0)
        + core(speed_v, 1, 0)
    ) / 16.0
    new_u = across / (2.0 * mean_depth) + smooth_u
    new_v = along / (2.0 * mean_depth) + smooth_v
    sediment = core(padded[2], 0, 0) + time_step * (
        middle(to_right, 0, -1) * middle(carried, 0, -1)
        + middle(to_left, 0, 1) * middle(carried, 0, 1)
        + middle(to_lower, -1, 0) * middle(carried, -1, 0)
        + middle(to_upper, 1, 0) * middle(carried, 1, 0)
        - outflow * middle(carried, 0, 0)
    )
    left_in = col_ok[1 : 1 + cols_out][None, :]
    right_in = col_ok[3 : 3 + cols_out][None, :]
    upper_in = row_ok[1 : 1 + rows_out][:, None]
    lower_in = row_ok[3 : 3 + rows_out][:, None]
    base = core(height, 0, 0)
    diff_left = core(height, 0, -1) - base
    diff_right = core(height, 0, 1) - base
    diff_upper = core(height, -1, 0) - base
    diff_lower = core(height, 1, 0) - base
    grad_x = 0.5 * (right_in * diff_right - left_in * diff_left)
    grad_y = 0.5 * (lower_in * diff_lower - upper_in * diff_upper)
    grad_sq = grad_x * grad_x + grad_y * grad_y
    capacity = carry_coef * jnp.sqrt(
        (new_u * new_u + new_v * new_v) * grad_sq / (1.0 + grad_sq) + cap_floor
    )
    gap_left = capacity - sediment
    delta = jnp.where(gap_left > 0.0, erode_coef * erod * gap_left, settle_coef * gap_left)
    thermal = slide_coef * (
        left_in * talus_flow(diff_left)
        + right_in * talus_flow(diff_right)
        + upper_in * talus_flow(diff_upper)
        + lower_in * talus_flow(diff_lower)
    )
    new_height = base - delta + thermal
    new_sediment = sediment + delta
    out_ok = row_ok[2 : 2 + rows_out][:, None] * col_ok[2 : 2 + cols_out][None, :]
    fresh = jnp.stack(
        [
            new_height,
            water_new,
            new_sediment,
            middle(to_left, 0, 0),
            middle(to_right, 0, 0),
            middle(to_upper, 0, 0),
            middle(to_lower, 0, 0),
            new_u,
            new_v,
        ]
    )
    return fresh * out_ok[None], water_new


def settle(fresh, rain_field, mean_water):
    return fresh.at[1].set(fresh[1] * (1.0 - evap_coef * mean_water) + rain_depth * rain_field)


def valid_line(index, extent, whole, margin):
    places = index * extent + jnp.arange(-margin, extent + margin, dtype=jnp.int32)
    return ((places >= 0) & (places < whole)).astype(jnp.float32)


def flip_pairs(count, partner):
    return [(i, partner(i)) for i in range(count)]


def quad_pairs(count, stride, shift):
    return [
        (i, i - ((i // stride) % 4) * stride + (((i // stride) % 4 + shift) % 4) * stride)
        for i in range(count)
    ]


def butterfly_sum(value):
    rows = lax.axis_size("rows")
    cols = lax.axis_size("cols")
    total = jnp.broadcast_to(value, (1, 128))
    part = total
    for flip_r, flip_c in ((0, 1), (4, 0), (4, 1)):
        pairs = [(r * cols + c, (r ^ flip_r) * cols + (c ^ flip_c)) for r in range(rows) for c in range(cols)]
        part = part + lax.ppermute(total, ("rows", "cols"), pairs)
    total = part
    for axis, count, stride in (("rows", rows, 1), ("rows", rows, 8), ("cols", cols, 2)):
        part = total
        for shift in (1, 3, 2):
            if axis == "cols" and shift == 2:
                pairs = [(r * cols + c, opposite_z(r, c, cols)) for r in range(rows) for c in range(cols)]
                part = part + lax.ppermute(total, ("rows", "cols"), pairs)
                continue
            part = part + lax.ppermute(total, axis, quad_pairs(count, stride, shift))
        total = part
    return total[0, 0]


def opposite_z(r, c, cols):
    z_lo, z_hi = (r // 4) % 2, c // 2
    z = 2 * z_hi + z_lo
    other = (5 - z) % 8 if z_hi % 2 == 0 else (9 - z) % 8
    return (r - 4 * z_lo + 4 * (other % 2)) * cols + 2 * (other // 2) + c % 2


def shards(state, hardness, rain_mask):
    rows_own = state.shape[1]
    cols_own = state.shape[2]
    whole_rows = rows_own * lax.axis_size("rows")
    whole_cols = cols_own * lax.axis_size("cols")
    cells = float(whole_rows * whole_cols)
    row_index = lax.axis_index("rows")
    col_index = lax.axis_index("cols")
    erod_own = rock_rate(hardness)
    rain_own = rain_mask.astype(jnp.float32)
    width = 2 * STEPS
    stacked = jnp.concatenate([state, erod_own[None], rain_own[None]], axis=0)
    stacked = with_halo(stacked, (("rows", 1), ("cols", 2)), width)
    current = stacked[:9]
    erod_ext = stacked[9]
    rain_ext = stacked[10]
    row_ok = valid_line(row_index, rows_own, whole_rows, width)
    col_ok = valid_line(col_index, cols_own, whole_cols, width)
    for step in range(STEPS):
        margin = width - 2 * step
        cut = 2 * step
        row_ok_now = row_ok[cut : cut + rows_own + 2 * margin]
        col_ok_now = col_ok[cut : cut + cols_own + 2 * margin]
        inner_cut = cut + 2
        out_rows = rows_own + 2 * margin - 4
        out_cols = cols_own + 2 * margin - 4
        erod_now = erod_ext[inner_cut : inner_cut + out_rows, inner_cut : inner_cut + out_cols]
        rain_now = rain_ext[inner_cut : inner_cut + out_rows, inner_cut : inner_cut + out_cols]
        fresh, water_new = advance(current, erod_now, row_ok_now, col_ok_now)
        keep = margin - 2
        own_water = water_new[keep : keep + rows_own, keep : keep + cols_own]
        mean_water = butterfly_sum(jnp.sum(own_water * own_water)) / cells
        current = settle(fresh, rain_now, mean_water)
    return current


def solution(mesh):
    in_specs = (P(None, "rows", "cols"), P("rows", "cols"), P("rows", "cols"))
    out_specs = P(None, "rows", "cols")
    return jax.shard_map(shards, mesh=mesh, in_specs=in_specs, out_specs=out_specs, check_vma=False)
```
